256 devices in a mesh: section: 2 (over core), seq: 32 (over z, x), cfg: 4 (over y).
Axes of the slice: x: 4, y: 4, z: 8, core: 2. Of those that a mesh axis runs over, the one named last changes fastest.
Arguments:
- hidden_states: bfloat16 [4, 4, 512, 3072], P('cfg', None, 'seq'), may hold values from -250 to 250
- latent: float32 [2, 4, 512, 64], P('section', None, 'seq'), may hold values from -6 to 6
- stale_cache: bfloat16 [2, 4, 32, 2048, 128], P('section', 'cfg', 'seq'), may hold values from -140 to 140
- qkv_weight: bfloat16 [2, 3072, 3, 2048], P('section', None, None, 'cfg'), may hold values from -0.109375 to 0.109375
- out_weight: bfloat16 [2, 3072, 2048], P('section', 'seq', 'cfg'), may hold values from -0.125 to 0.125
- modulation: float32 [2, 6, 3072], P('section'), may hold values from -2.5 to 2.5
- out_modulation: float32 [2, 3072], replicated, may hold values from -2.5 to 2.5
- proj_weight: bfloat16 [3072, 64], replicated, may hold values from -0.109375 to 0.109375
- solver_coef: float32 [2, 3], P('section'), may hold values from 0.5 to 2
- video_len: int32 [2], replicated, may hold values from 911 to 1822, as said below
- text_len: int32 [4], replicated, may hold values from 1 to 226, as said below
- positions: int32 [3, 2, 4, 512], P(None, None, None, 'seq'), may hold values from 0 to 47
Outputs:
- new_latent: float32 [2, 4, 512, 64], P('section', None, 'seq')
- new_cache: bfloat16 [2, 4, 32, 2048, 128], P('section', 'cfg', 'seq')
The draws below stay inside these ranges and needn't reach their ends.
Inputs may be any that keep to these rules, and one draw needn't show every extreme that they name: `video_len`: in every draw one request has exactly 1822 video tokens. `text_len`: in every draw some sequence has all 226 text tokens live.
All inputs are finite; a program needn't handle non-finite values.
Results may differ from the reference program's by a relative error of at most 0.02.
Values may be sent and summed in bfloat16 or wider, within the bound.
No kernel may reach another device: no remote copies, remote signals or barrier semaphores. Data moves between devices by JAX's collectives and lax.ppermute only.
A program may use at most 128 MiB of HBM per device.

```python
import math
import jax
import jax.numpy as jnp
from jax import lax

D = 3072
HD = 64
TEXT = 226
OUT = 64
PATCHES = 4
REQS = 2
SEQS = 4
SECTIONS = 2
PATCH_LEN = 512
SEQ = 2048
HEADS = 32
ATT = 2048
GROUPS = 4
PAIRS = 32
N_SEQ = 32
N_CFG = 4


def draw_hidden_states(key, part):
    subkeys = jax.random.split(key, 1)
    shape = (SEQS, PATCHES, PATCH_LEN, D)
    values = jnp.clip(jax.random.normal(subkeys[0], shape, jnp.float32), -6.0, 6.0) * 0.2
    return values.astype(jnp.bfloat16)


def draw_stale_cache(key, part):
    subkeys = jax.random.split(key, 1)
    shape = (SECTIONS, GROUPS, PAIRS, SEQ, 2 * HD)
    values = jnp.clip(jax.random.normal(subkeys[0], shape, jnp.float32), -6.0, 6.0)
    return values.astype(jnp.bfloat16)


def draw_video_len(key, part):
    subkeys = jax.random.split(key, 2)
    longest = SEQ - TEXT
    others = jax.random.randint(subkeys[0], (REQS,), longest // 2, longest + 1)
    which_one = jax.random.randint(subkeys[1], (), 0, REQS)
    return jnp.where(jnp.arange(REQS) == which_one, longest, others).astype(jnp.int32)


def draw_text_len(key, part):
    subkeys = jax.random.split(key, 2)
    others = jax.random.randint(subkeys[0], (SEQS,), 1, TEXT + 1)
    which_one = jax.random.randint(subkeys[1], (), 0, SEQS)
    return jnp.where(jnp.arange(SEQS) == which_one, TEXT, others).astype(jnp.int32)


def place_ends(result, rng, least, high):
    longest = result.shape.index(max(result.shape))
    spots = []
    for shift in (0, 1):
        where = [jax.random.randint(jax.random.fold_in(rng, axis), (), 0, length) for axis, length in enumerate(result.shape)]
        where[longest] = (where[longest] + shift) % result.shape[longest]
        spots.append(tuple(where))
    return result.at[spots[0]].set(least).at[spots[1]].set(high)


def block_scale(key, shape, pieces, low, largest):
    level = 1.0
    for axis_at, blocks in pieces:
        draws = jax.random.uniform(jax.random.fold_in(jax.random.fold_in(key, 6), axis_at), (blocks,), jnp.float32, low / len(pieces), largest / len(pieces))
        level = level * jnp.repeat(jnp.exp(draws), shape[axis_at] // blocks).reshape((-1,) + (1,) * (len(shape) - 1 - axis_at))
    return level


def gaussian(stream_key, shape, width, reach, shards=(), held_as=jnp.bfloat16):
    entries = jax.random.normal(stream_key, shape, jnp.float32) * width
    if len(shards) > 0:
        entries = block_scale(stream_key, shape, shards, -0.22, 0.18) * entries
    return jnp.clip(entries, min=-reach, max=reach).astype(held_as)


def setup_inputs(seed: int = 0) -> dict:
    key_of = jax.random.split(jax.random.key(seed), 13)
    hidden_states = draw_hidden_states(jax.random.fold_in(key_of[12], 71), 0)
    latent = gaussian(key_of[1], (REQS, PATCHES, PATCH_LEN, OUT), 1.0, 6.0, ((0, 2), (2, 32)), jnp.float32)
    stale_cache = draw_stale_cache(jax.random.fold_in(key_of[12], 71), 0)
    qkv_weight = gaussian(key_of[3], (SECTIONS, D, 3, ATT), D ** -0.5, 0.109375, ((0, 2), (3, 4)))
    out_weight = gaussian(key_of[4], (SECTIONS, D, ATT), ATT ** -0.5, 0.125, ((0, 2), (1, 32), (2, 4)))
    modulation = gaussian(key_of[5], (SECTIONS, 6, D), 0.5, 2.5, ((0, 2),), jnp.float32)
    out_modulation = gaussian(key_of[6], (2, D), 0.5, 2.5, (), jnp.float32)
    proj_weight = gaussian(key_of[7], (D, OUT), D ** -0.5, 0.109375)
    solver_coef = jnp.clip(0.5 + 1.5 * jax.random.uniform(key_of[8], (REQS, 3), jnp.float32) ** block_scale(key_of[8], (REQS, 3), ((0, 2),), -0.2, 0.2), 0.5, 2.0)
    video_len = draw_video_len(jax.random.fold_in(key_of[12], 71), 0)
    text_len = draw_text_len(jax.random.fold_in(key_of[12], 71), 0)
    positions = place_ends(jax.random.randint(key_of[11], (3, REQS, PATCHES, PATCH_LEN), 0, 48), jax.random.fold_in(key_of[11], 1), 0, 47).astype(jnp.int32)
    return dict(hidden_states=hidden_states, latent=latent, stale_cache=stale_cache, qkv_weight=qkv_weight, out_weight=out_weight, modulation=modulation, out_modulation=out_modulation, proj_weight=proj_weight, solver_coef=solver_coef, video_len=video_len, text_len=text_len, positions=positions)


def row_norm(values):
    centered = values - lax.optimization_barrier(jnp.mean(values, axis=-1, keepdims=True))
    return centered * lax.rsqrt(lax.optimization_barrier(jnp.mean(centered * centered, axis=-1, keepdims=True)) + 1e-05)

def head_norm(values):
    centered = values - lax.optimization_barrier(jnp.mean(values, axis=-1, keepdims=True))
    return centered * lax.rsqrt(lax.optimization_barrier(jnp.mean(centered * centered, axis=-1, keepdims=True)) + 1e-06)

def rope_angles(places, head_size):
    half_size = head_size // 2
    pairs_t = head_size // 8
    pairs_h = (half_size - pairs_t) // 2
    pair_index = jnp.arange(half_size)
    first_part = pair_index < pairs_t
    second_part = jnp.logical_and(pair_index >= pairs_t, pair_index < pairs_t + pairs_h)
    third_part = pair_index >= pairs_t + pairs_h
    local_index = jnp.where(first_part, pair_index, jnp.where(second_part, pair_index - pairs_t, pair_index - pairs_t - pairs_h))
    axis_span = jnp.where(first_part, 2 * pairs_t, 2 * pairs_h)
    frequency = jnp.exp(-math.log(10000.0) * 2.0 * local_index.astype(jnp.float32) / axis_span.astype(jnp.float32))
    angles = places[0][..., None] * first_part.astype(jnp.float32)
    angles = angles + places[1][..., None] * second_part.astype(jnp.float32)
    angles = angles + places[2][..., None] * third_part.astype(jnp.float32)
    return angles * frequency

def rotate(values, cos_table, sin_table):
    half_size = values.shape[-1] // 2
    first_half = values[..., :half_size]
    second_half = values[..., half_size:]
    return jnp.concatenate([first_half * cos_table - second_half * sin_table, second_half * cos_table + first_half * sin_table], axis=-1)

def attend_pair(work_item):
    fresh_one, stale_one, query_one, live_one = work_item
    key_patch = jnp.arange(SEQ) // PATCH_LEN
    outputs = []
    for patch_id in range(PATCHES):
        key_rows = jnp.where((key_patch <= patch_id)[:, None], fresh_one, stale_one)
        query_block = query_one[patch_id * PATCH_LEN:(patch_id + 1) * PATCH_LEN]
        scores = jnp.dot(query_block, key_rows[:, :HD].T, preferred_element_type=jnp.float32) * HD ** (-0.5)
        scores = jnp.where(live_one[None, :], scores, -jnp.inf)
        row_max = lax.optimization_barrier(jnp.max(scores, axis=1, keepdims=True))
        weights = jnp.exp(scores - row_max)
        row_sum = lax.optimization_barrier(jnp.sum(weights, axis=1, keepdims=True))
        combined = jnp.dot(weights.astype(jnp.bfloat16), key_rows[:, HD:], preferred_element_type=jnp.float32)
        outputs.append((combined / row_sum).astype(jnp.bfloat16))
    return jnp.concatenate(outputs, axis=0)

def reference(hidden_states, latent, stale_cache, qkv_weight, out_weight, modulation, out_modulation, proj_weight, solver_coef, video_len, text_len, positions):
    row_ids = jnp.arange(SEQ)
    text_rows = row_ids < TEXT
    video_rep = jnp.repeat(video_len, 2)
    live_keys = jnp.where(text_rows[None, :], row_ids[None, :] < text_len[:, None], row_ids[None, :] - TEXT < video_rep[:, None])
    places = positions.reshape(3, REQS, SEQ).astype(jnp.float32)
    angles = rope_angles(places, HD)
    angles = jnp.where(text_rows[None, :, None], 0.0, angles)
    angles = jnp.repeat(angles, 2, axis=0)
    cos_table = jnp.cos(angles)[:, :, None, :]
    sin_table = jnp.sin(angles)[:, :, None, :]
    group_heads = HEADS // N_CFG
    hidden = hidden_states.reshape(SEQS, SEQ, D)
    caches = []
    for section_id in range(SECTIONS):
        mod_rows = modulation[section_id]
        normed = row_norm(hidden.astype(jnp.float32))
        shift_rows = jnp.where(text_rows[:, None], mod_rows[3], mod_rows[0])
        scale_rows = jnp.where(text_rows[:, None], mod_rows[4], mod_rows[1])
        gate_rows = jnp.where(text_rows[:, None], mod_rows[5], mod_rows[2])
        mixed_rows = (normed * (1.0 + scale_rows) + shift_rows).astype(jnp.bfloat16)
        projected = jnp.dot(mixed_rows.reshape(SEQS * SEQ, D), qkv_weight[section_id].reshape(D, 3 * ATT), preferred_element_type=jnp.float32)
        projected = projected.reshape(SEQS, SEQ, 3, HEADS, HD)
        queries = rotate(head_norm(projected[:, :, 0]), cos_table, sin_table).astype(jnp.bfloat16)
        key_part = rotate(head_norm(projected[:, :, 1]), cos_table, sin_table).astype(jnp.bfloat16)
        value_part = projected[:, :, 2].astype(jnp.bfloat16)
        fresh_rows = jnp.concatenate([key_part, value_part], axis=-1).transpose(0, 2, 1, 3)
        stale_rows = stale_cache[section_id].reshape(N_CFG, SEQS, group_heads, SEQ, 2 * HD).transpose(1, 0, 2, 3, 4).reshape(SEQS, HEADS, SEQ, 2 * HD)
        query_rows = queries.transpose(0, 2, 1, 3).reshape(SEQS * HEADS, SEQ, HD)
        live_rep = jnp.repeat(live_keys, HEADS, axis=0)
        attended = lax.map(attend_pair, (fresh_rows.reshape(SEQS * HEADS, SEQ, 2 * HD), stale_rows.reshape(SEQS * HEADS, SEQ, 2 * HD), query_rows, live_rep))
        attended = attended.reshape(SEQS, HEADS, SEQ, HD).transpose(0, 2, 1, 3).reshape(SEQS * SEQ, ATT)
        update = jnp.dot(attended, out_weight[section_id].T, preferred_element_type=jnp.float32).reshape(SEQS, SEQ, D)
        hidden = (hidden.astype(jnp.float32) + gate_rows * update).astype(jnp.bfloat16)
        caches.append(fresh_rows.reshape(SEQS, N_CFG, group_heads, SEQ, 2 * HD).transpose(1, 0, 2, 3, 4).reshape(N_CFG, N_SEQ, SEQ, 2 * HD))
    normed = row_norm(hidden.astype(jnp.float32))
    normed_out = (normed * (1.0 + out_modulation[1]) + out_modulation[0]).astype(jnp.bfloat16)
    predicted = jnp.dot(normed_out.reshape(SEQS * SEQ, D), proj_weight, preferred_element_type=jnp.float32).reshape(REQS, 2, SEQ, OUT)
    guide_scale = solver_coef[:, 2][:, None, None]
    guided = predicted[:, 0] + guide_scale * (predicted[:, 1] - predicted[:, 0])
    latent_rows = latent.reshape(REQS, SEQ, OUT)
    new_latent = solver_coef[:, 0][:, None, None] * latent_rows + solver_coef[:, 1][:, None, None] * guided
    return (new_latent.reshape(REQS, PATCHES, PATCH_LEN, OUT), jnp.stack(caches, axis=0))
```

```python
import math

import jax
import jax.numpy as jnp
from jax import lax
from jax.sharding import PartitionSpec as P

HD = 64
TEXT = 226


def from_behind(value, axis, steps):
    count = lax.axis_size(axis)
    pairs = [(source, (source + steps) % count) for source in range(count)]
    return lax.ppermute(value, axis, pairs)


def row_norm(values):
    centered = values - jnp.mean(values, axis=-1, keepdims=True)
    return centered * lax.rsqrt(jnp.mean(centered * centered, axis=-1, keepdims=True) + 1e-05)


def head_norm(values):
    centered = values - jnp.mean(values, axis=-1, keepdims=True)
    return centered * lax.rsqrt(jnp.mean(centered * centered, axis=-1, keepdims=True) + 1e-06)


def rope_angles(places, head_size):
    half_size = head_size // 2
    pairs_t = head_size // 8
    pairs_h = (half_size - pairs_t) // 2
    pair_index = jnp.arange(half_size)
    first_part = pair_index < pairs_t
    second_part = jnp.logical_and(pair_index >= pairs_t, pair_index < pairs_t + pairs_h)
    third_part = pair_index >= pairs_t + pairs_h
    local_index = jnp.where(
        first_part,
        pair_index,
        jnp.where(second_part, pair_index - pairs_t, pair_index - pairs_t - pairs_h),
    )
    axis_span = jnp.where(first_part, 2 * pairs_t, 2 * pairs_h)
    frequency = jnp.exp(
        -math.log(10000.0) * 2.0 * local_index.astype(jnp.float32) / axis_span.astype(jnp.float32)
    )
    angles = places[0][..., None] * first_part.astype(jnp.float32)
    angles = angles + places[1][..., None] * second_part.astype(jnp.float32)
    angles = angles + places[2][..., None] * third_part.astype(jnp.float32)
    return angles * frequency


def rotate(values, cos_table, sin_table):
    half_size = values.shape[-1] // 2
    first_half = values[..., :half_size]
    second_half = values[..., half_size:]
    return jnp.concatenate(
        [
            first_half * cos_table - second_half * sin_table,
            second_half * cos_table + first_half * sin_table,
        ],
        axis=-1,
    )


def per_device(
    hidden_states,
    latent,
    stale_cache,
    qkv_weight,
    out_weight,
    modulation,
    out_modulation,
    proj_weight,
    solver_coef,
    video_len,
    text_len,
    positions,
):
    section_id = lax.axis_index("section")
    shard_id = lax.axis_index("seq")
    seq_devices = lax.axis_size("seq")
    cfg_devices = lax.axis_size("cfg")
    patches = hidden_states.shape[1]
    patch_dev = hidden_states.shape[2]
    width = hidden_states.shape[3]
    patch_len = patch_dev * seq_devices
    total_len = patch_len * patches
    group_heads = qkv_weight.shape[3] // HD
    seq_count = cfg_devices
    qkv_full = qkv_weight[0].reshape(width, 3, group_heads, HD)
    out_full = lax.all_gather(out_weight[0], "seq", axis=0, tiled=True).reshape(
        width, group_heads, HD
    )
    mod_rows = modulation[0]
    stale_rows = stale_cache[0, 0, 0]
    my_sequence = shard_id // group_heads
    row_ids = jnp.arange(total_len)
    text_limit = lax.dynamic_index_in_dim(text_len, my_sequence, keepdims=False)
    video_limit = lax.dynamic_index_in_dim(video_len, my_sequence // 2, keepdims=False)
    live_keys = jnp.where(row_ids < TEXT, row_ids < text_limit, row_ids - TEXT < video_limit)
    key_patch = row_ids // patch_len
    use_fresh = key_patch[None, :] <= jnp.arange(patches)[:, None]
    scale_factor = HD ** (-0.5)

    row_place = (
        jnp.arange(patches)[:, None] * patch_len
        + shard_id * patch_dev
        + jnp.arange(patch_dev)[None, :]
    )
    text_rows = (row_place < TEXT)[:, :, None]
    shift_rows = jnp.where(text_rows, mod_rows[3], mod_rows[0])
    scale_rows = jnp.where(text_rows, mod_rows[4], mod_rows[1])
    gate_rows = jnp.where(text_rows, mod_rows[5], mod_rows[2])
    angles = rope_angles(positions.astype(jnp.float32), HD)
    angles = jnp.where(text_rows[None], 0.0, angles)
    angles = jnp.repeat(angles, 2, axis=0)[:, None]
    cos_table = jnp.cos(angles)
    sin_table = jnp.sin(angles)

    def run(hidden):
        normed = row_norm(hidden.astype(jnp.float32))
        mixed_rows = (normed * (1.0 + scale_rows) + shift_rows).astype(jnp.bfloat16)
        mixed_rows = lax.all_gather(mixed_rows, "cfg", axis=0, tiled=True)
        projected = jnp.einsum(
            "spqd,djge->sgjpqe", mixed_rows, qkv_full, preferred_element_type=jnp.float32
        )
        queries = rotate(head_norm(projected[:, :, 0]), cos_table, sin_table)
        key_part = rotate(head_norm(projected[:, :, 1]), cos_table, sin_table)
        stacked = jnp.stack([queries, key_part, projected[:, :, 2]], axis=2).astype(jnp.bfloat16)
        outgoing = stacked.reshape(seq_count * group_heads, 3, patches, patch_dev * HD)
        incoming = lax.all_to_all(outgoing, "seq", split_axis=0, concat_axis=3, tiled=True)
        incoming = incoming.reshape(3, patches, patch_len, HD)
        fresh_rows = jnp.concatenate([incoming[1], incoming[2]], axis=-1).reshape(
            total_len, 2 * HD
        )
        key_rows = jnp.where(use_fresh[:, :, None], fresh_rows[None], stale_rows[None])
        scores = (
            jnp.einsum(
                "pqe,pke->pqk", incoming[0], key_rows[..., :HD], preferred_element_type=jnp.float32
            )
            * scale_factor
        )
        scores = jnp.where(live_keys[None, None, :], scores, -jnp.inf)
        row_max = jnp.max(scores, axis=-1, keepdims=True)
        weights = jnp.exp(scores - row_max)
        row_sum = jnp.sum(weights, axis=-1, keepdims=True)
        combined = jnp.einsum(
            "pqk,pke->pqe",
            weights.astype(jnp.bfloat16),
            key_rows[..., HD:],
            preferred_element_type=jnp.float32,
        )
        attended = (combined / row_sum).astype(jnp.bfloat16)
        attended = attended.reshape(patches, seq_devices, patch_dev * HD)[None]
        returned = lax.all_to_all(attended, "seq", split_axis=2, concat_axis=0, tiled=True)
        returned = returned.reshape(seq_count, group_heads, patches, patch_dev, HD)
        update = lax.psum_scatter(
            jnp.einsum("sgpqe,dge->spqd", returned, out_full, preferred_element_type=jnp.float32),
            "cfg",
            scatter_dimension=0,
            tiled=True,
        )
        result = (hidden.astype(jnp.float32) + gate_rows * update).astype(jnp.bfloat16)
        return result, fresh_rows

    first_out, first_cache = run(hidden_states)
    received = from_behind(first_out, "section", 1)
    second_out, second_cache = run(received)
    key_cache = jnp.where(section_id == 0, first_cache, second_cache)

    normed = row_norm(second_out.astype(jnp.float32))
    normed_out = (normed * (1.0 + out_modulation[1]) + out_modulation[0]).astype(jnp.bfloat16)
    predicted = jnp.einsum(
        "spqd,do->spqo", normed_out, proj_weight, preferred_element_type=jnp.float32
    )
    predicted_all = lax.all_gather(predicted, ("section", "cfg"), axis=0, tiled=True)
    predicted_all = predicted_all[predicted_all.shape[0] - seq_count :]
    pair_rows = lax.dynamic_slice_in_dim(predicted_all, 2 * section_id, 2, 0)
    solver_row = solver_coef[0]
    guided = pair_rows[0] + solver_row[2] * (pair_rows[1] - pair_rows[0])
    new_latent = solver_row[0] * latent[0] + solver_row[1] * guided
    return (new_latent[None], key_cache[None, None, None])


def solution(mesh):
    return jax.shard_map(
        per_device,
        mesh=mesh,
        in_specs=(
            P("cfg", None, "seq", None),
            P("section", None, "seq", None),
            P("section", "cfg", "seq", None, None),
            P("section", None, None, "cfg"),
            P("section", "seq", "cfg"),
            P("section", None, None),
            P(),
            P(),
            P("section", None),
            P(),
            P(),
            P(None, None, None, "seq"),
        ),
        out_specs=(P("section", None, "seq", None), P("section", "cfg", "seq", None, None)),
        check_vma=False,
    )
```

```python
import math

import jax
import jax.numpy as jnp
from jax import lax
from jax.sharding import PartitionSpec as P

HD = 64
TEXT = 226


def from_behind(value, axis, steps):
    count = lax.axis_size(axis)
    pairs = [(source, (source + steps) % count) for source in range(count)]
    return lax.ppermute(value, axis, pairs)


def row_norm(values):
    centered = values - jnp.mean(values, axis=-1, keepdims=True)
    return centered * lax.rsqrt(jnp.mean(centered * centered, axis=-1, keepdims=True) + 1e-05)


def head_norm(values):
    centered = values - jnp.mean(values, axis=-1, keepdims=True)
    return centered * lax.rsqrt(jnp.mean(centered * centered, axis=-1, keepdims=True) + 1e-06)


def rope_angles(places, head_size):
    half_size = head_size // 2
    pairs_t = head_size // 8
    pairs_h = (half_size - pairs_t) // 2
    pair_index = jnp.arange(half_size)
    first_part = pair_index < pairs_t
    second_part = jnp.logical_and(pair_index >= pairs_t, pair_index < pairs_t + pairs_h)
    third_part = pair_index >= pairs_t + pairs_h
    local_index = jnp.where(
        first_part,
        pair_index,
        jnp.where(second_part, pair_index - pairs_t, pair_index - pairs_t - pairs_h),
    )
    axis_span = jnp.where(first_part, 2 * pairs_t, 2 * pairs_h)
    frequency = jnp.exp(
        -math.log(10000.0) * 2.0 * local_index.astype(jnp.float32) / axis_span.astype(jnp.float32)
    )
    angles = places[0][..., None] * first_part.astype(jnp.float32)
    angles = angles + places[1][..., None] * second_part.astype(jnp.float32)
    angles = angles + places[2][..., None] * third_part.astype(jnp.float32)
    return angles * frequency


def rotate(values, cos_table, sin_table):
    half_size = values.shape[-1] // 2
    first_half = values[..., :half_size]
    second_half = values[..., half_size:]
    return jnp.concatenate(
        [
            first_half * cos_table - second_half * sin_table,
            second_half * cos_table + first_half * sin_table,
        ],
        axis=-1,
    )


def gather_cfg(values):
    count = lax.axis_size("cfg")
    here = lax.axis_index("cfg")
    slots = [values] + [from_behind(values, "cfg", shift) for shift in range(1, count)]
    ordered = jnp.concatenate(slots[::-1], axis=0)
    return jnp.roll(ordered, here + 1, axis=0)


def scatter_cfg(partials):
    count = lax.axis_size("cfg")
    here = lax.axis_index("cfg")
    total = lax.dynamic_index_in_dim(partials, here, 0, keepdims=True)
    for shift in range(1, count):
        outgoing = lax.dynamic_index_in_dim(partials, (here + shift) % count, 0, keepdims=True)
        total = total + from_behind(outgoing, "cfg", shift)
    return total


def per_device(
    hidden_states,
    latent,
    stale_cache,
    qkv_weight,
    out_weight,
    modulation,
    out_modulation,
    proj_weight,
    solver_coef,
    video_len,
    text_len,
    positions,
):
    section_id = lax.axis_index("section")
    shard_id = lax.axis_index("seq")
    seq_devices = lax.axis_size("seq")
    cfg_devices = lax.axis_size("cfg")
    patches = hidden_states.shape[1]
    patch_dev = hidden_states.shape[2]
    width = hidden_states.shape[3]
    patch_len = patch_dev * seq_devices
    total_len = patch_len * patches
    group_heads = qkv_weight.shape[3] // HD
    seq_count = cfg_devices
    qkv_full = qkv_weight[0].reshape(width, 3 * group_heads * HD)
    out_full = lax.all_gather(out_weight[0], "seq", axis=0, tiled=True).reshape(
        width, group_heads, HD
    )
    mod_rows = modulation[0]
    stale_rows = stale_cache[0, 0, 0]
    my_sequence = shard_id // group_heads
    row_ids = jnp.arange(total_len)
    text_limit = lax.dynamic_index_in_dim(text_len, my_sequence, keepdims=False)
    video_limit = lax.dynamic_index_in_dim(video_len, my_sequence // 2, keepdims=False)
    live_keys = jnp.where(row_ids < TEXT, row_ids < text_limit, row_ids - TEXT < video_limit)
    key_patch = row_ids // patch_len
    use_fresh = key_patch[None, :] <= jnp.arange(patches)[:, None]
    scale_factor = HD ** (-0.5)

    row_place = (
        jnp.arange(patches)[:, None] * patch_len
        + shard_id * patch_dev
        + jnp.arange(patch_dev)[None, :]
    )
    text_rows = (row_place < TEXT)[:, :, None]
    shift_rows = jnp.where(text_rows, mod_rows[3], mod_rows[0])
    scale_rows = jnp.where(text_rows, mod_rows[4], mod_rows[1])
    gate_rows = jnp.where(text_rows, mod_rows[5], mod_rows[2])
    angles = rope_angles(positions.astype(jnp.float32), HD)
    angles = jnp.where(text_rows[None], 0.0, angles)
    angles = jnp.repeat(angles, 2, axis=0)[:, None]
    cos_table = jnp.cos(angles)
    sin_table = jnp.sin(angles)

    def run(hidden):
        normed = row_norm(hidden.astype(jnp.float32))
        mixed_rows = (normed * (1.0 + scale_rows) + shift_rows).astype(jnp.bfloat16)
        mixed_rows = gather_cfg(mixed_rows)
        projected = jnp.dot(
            mixed_rows.reshape(-1, width), qkv_full, preferred_element_type=jnp.float32
        )
        projected = projected.reshape(seq_count, patches, patch_dev, 3, group_heads, HD)
        projected = projected.transpose(0, 4, 3, 1, 2, 5)
        queries = rotate(head_norm(projected[:, :, 0]), cos_table, sin_table)
        key_part = rotate(head_norm(projected[:, :, 1]), cos_table, sin_table)
        stacked = jnp.stack([queries, key_part, projected[:, :, 2]], axis=2).astype(jnp.bfloat16)
        outgoing = stacked.reshape(seq_count * group_heads, 3, patches, patch_dev * HD)
        incoming = lax.all_to_all(outgoing, "seq", split_axis=0, concat_axis=3, tiled=True)
        incoming = incoming.reshape(3, patches, patch_len, HD)
        fresh_rows = jnp.concatenate([incoming[1], incoming[2]], axis=-1).reshape(
            total_len, 2 * HD
        )
        key_rows = jnp.where(use_fresh[:, :, None], fresh_rows[None], stale_rows[None])
        scores = (
            jnp.einsum(
                "pqe,pke->pqk", incoming[0], key_rows[..., :HD], preferred_element_type=jnp.float32
            )
            * scale_factor
        )
        scores = jnp.where(live_keys[None, None, :], scores, -jnp.inf)
        row_max = jnp.max(scores, axis=-1, keepdims=True)
        weights = jnp.exp(scores - row_max)
        row_sum = jnp.sum(weights, axis=-1, keepdims=True)
        combined = jnp.einsum(
            "pqk,pke->pqe",
            weights.astype(jnp.bfloat16),
            key_rows[..., HD:],
            preferred_element_type=jnp.float32,
        )
        attended = (combined / row_sum).astype(jnp.bfloat16)
        attended = attended.reshape(patches, seq_devices, patch_dev * HD)[None]
        returned = lax.all_to_all(attended, "seq", split_axis=2, concat_axis=0, tiled=True)
        returned = returned.reshape(seq_count, group_heads, patches, patch_dev, HD)
        update = scatter_cfg(
            jnp.einsum("sgpqe,dge->spqd", returned, out_full, preferred_element_type=jnp.float32)
        )
        result = (hidden.astype(jnp.float32) + gate_rows * update).astype(jnp.bfloat16)
        return result, fresh_rows

    first_out, first_cache = run(hidden_states)
    received = from_behind(first_out, "section", 1)
    second_out, second_cache = run(received)
    key_cache = jnp.where(section_id == 0, first_cache, second_cache)

    normed = row_norm(second_out.astype(jnp.float32))
    normed_out = (normed * (1.0 + out_modulation[1]) + out_modulation[0]).astype(jnp.bfloat16)
    predicted = jnp.einsum(
        "spqd,do->spqo", normed_out, proj_weight, preferred_element_type=jnp.float32
    )
    predicted_all = gather_cfg(predicted)
    predicted_all = jnp.where(
        section_id == 0, from_behind(predicted_all, "section", 1), predicted_all
    )
    pair_rows = lax.dynamic_slice_in_dim(predicted_all, 2 * section_id, 2, 0)
    solver_row = solver_coef[0]
    guided = pair_rows[0] + solver_row[2] * (pair_rows[1] - pair_rows[0])
    new_latent = solver_row[0] * latent[0] + solver_row[1] * guided
    return (new_latent[None], key_cache[None, None, None])


def solution(mesh):
    return jax.shard_map(
        per_device,
        mesh=mesh,
        in_specs=(
            P("cfg", None, "seq", None),
            P("section", None, "seq", None),
            P("section", "cfg", "seq", None, None),
            P("section", None, None, "cfg"),
            P("section", "seq", "cfg"),
            P("section", None, None),
            P(),
            P(),
            P("section", None),
            P(),
            P(),
            P(None, None, None, "seq"),
        ),
        out_specs=(P("section", None, "seq", None), P("section", "cfg", "seq", None, None)),
        check_vma=False,
    )
```

```python
import math

import jax
import jax.numpy as jnp
from jax import lax
from jax.sharding import PartitionSpec as P

HD = 64
TEXT = 226


def from_behind(value, axis, steps):
    count = lax.axis_size(axis)
    pairs = [(source, (source + steps) % count) for source in range(count)]
    return lax.ppermute(value, axis, pairs)


def row_norm(values):
    centered = values - jnp.mean(values, axis=-1, keepdims=True)
    return centered * lax.rsqrt(jnp.mean(centered * centered, axis=-1, keepdims=True) + 1e-05)


def head_norm(values):
    centered = values - jnp.mean(values, axis=-1, keepdims=True)
    return centered * lax.rsqrt(jnp.mean(centered * centered, axis=-1, keepdims=True) + 1e-06)


def rope_angles(places, head_size):
    half_size = head_size // 2
    pairs_t = head_size // 8
    pairs_h = (half_size - pairs_t) // 2
    pair_index = jnp.arange(half_size)
    first_part = pair_index < pairs_t
    second_part = jnp.logical_and(pair_index >= pairs_t, pair_index < pairs_t + pairs_h)
    third_part = pair_index >= pairs_t + pairs_h
    local_index = jnp.where(
        first_part,
        pair_index,
        jnp.where(second_part, pair_index - pairs_t, pair_index - pairs_t - pairs_h),
    )
    axis_span = jnp.where(first_part, 2 * pairs_t, 2 * pairs_h)
    frequency = jnp.exp(
        -math.log(10000.0) * 2.0 * local_index.astype(jnp.float32) / axis_span.astype(jnp.float32)
    )
    angles = places[0][..., None] * first_part.astype(jnp.float32)
    angles = angles + places[1][..., None] * second_part.astype(jnp.float32)
    angles = angles + places[2][..., None] * third_part.astype(jnp.float32)
    return angles * frequency


def rotate(values, cos_table, sin_table):
    half_size = values.shape[-1] // 2
    first_half = values[..., :half_size]
    second_half = values[..., half_size:]
    return jnp.concatenate(
        [
            first_half * cos_table - second_half * sin_table,
            second_half * cos_table + first_half * sin_table,
        ],
        axis=-1,
    )


def shift_within(value, active, steps):
    count = lax.axis_size("cfg")
    pairs = [
        (active * count + source, active * count + (source + steps) % count)
        for source in range(count)
    ]
    return lax.ppermute(value, ("section", "cfg"), pairs)


def gather_cfg(values, active):
    count = lax.axis_size("cfg")
    here = lax.axis_index("cfg")
    slots = [values] + [shift_within(values, active, shift) for shift in range(1, count)]
    ordered = jnp.concatenate(slots[::-1], axis=0)
    return jnp.roll(ordered, here + 1, axis=0)


def scatter_cfg(partials, active):
    count = lax.axis_size("cfg")
    here = lax.axis_index("cfg")
    total = lax.dynamic_index_in_dim(partials, here, 0, keepdims=True)
    for shift in range(1, count):
        outgoing = lax.dynamic_index_in_dim(partials, (here + shift) % count, 0, keepdims=True)
        outgoing = outgoing.astype(jnp.bfloat16)
        total = total + shift_within(outgoing, active, shift).astype(jnp.float32)
    return total


def per_device(
    hidden_states,
    latent,
    stale_cache,
    qkv_weight,
    out_weight,
    modulation,
    out_modulation,
    proj_weight,
    solver_coef,
    video_len,
    text_len,
    positions,
):
    section_id = lax.axis_index("section")
    shard_id = lax.axis_index("seq")
    seq_devices = lax.axis_size("seq")
    cfg_devices = lax.axis_size("cfg")
    patches = hidden_states.shape[1]
    patch_dev = hidden_states.shape[2]
    width = hidden_states.shape[3]
    patch_len = patch_dev * seq_devices
    total_len = patch_len * patches
    group_heads = qkv_weight.shape[3] // HD
    seq_count = cfg_devices
    qkv_full = qkv_weight[0].reshape(width, 3 * group_heads * HD)
    out_full = lax.all_gather(out_weight[0], "seq", axis=0, tiled=True).reshape(
        width, group_heads, HD
    )
    mod_rows = modulation[0]
    stale_rows = stale_cache[0, 0, 0]
    my_sequence = shard_id // group_heads
    row_ids = jnp.arange(total_len)
    text_limit = lax.dynamic_index_in_dim(text_len, my_sequence, keepdims=False)
    video_limit = lax.dynamic_index_in_dim(video_len, my_sequence // 2, keepdims=False)
    live_keys = jnp.where(row_ids < TEXT, row_ids < text_limit, row_ids - TEXT < video_limit)
    key_patch = row_ids // patch_len
    use_fresh = key_patch[None, :] <= jnp.arange(patches)[:, None]
    scale_factor = HD ** (-0.5)

    row_place = (
        jnp.arange(patches)[:, None] * patch_len
        + shard_id * patch_dev
        + jnp.arange(patch_dev)[None, :]
    )
    text_rows = (row_place < TEXT)[:, :, None]
    shift_rows = jnp.where(text_rows, mod_rows[3], mod_rows[0])
    scale_rows = jnp.where(text_rows, mod_rows[4], mod_rows[1])
    gate_rows = jnp.where(text_rows, mod_rows[5], mod_rows[2])
    angles = rope_angles(positions.astype(jnp.float32), HD)
    angles = jnp.where(text_rows[None], 0.0, angles)
    angles = jnp.repeat(angles, 2, axis=0)[:, None]
    cos_table = jnp.cos(angles)
    sin_table = jnp.sin(angles)

    def run(hidden, active):
        normed = row_norm(hidden.astype(jnp.float32))
        mixed_rows = (normed * (1.0 + scale_rows) + shift_rows).astype(jnp.bfloat16)
        mixed_rows = gather_cfg(mixed_rows, active)
        projected = jnp.dot(
            mixed_rows.reshape(-1, width), qkv_full, preferred_element_type=jnp.float32
        )
        projected = projected.reshape(seq_count, patches, patch_dev, 3, group_heads, HD)
        projected = projected.transpose(0, 4, 3, 1, 2, 5)
        queries = rotate(head_norm(projected[:, :, 0]), cos_table, sin_table)
        key_part = rotate(head_norm(projected[:, :, 1]), cos_table, sin_table)
        stacked = jnp.stack([queries, key_part, projected[:, :, 2]], axis=2).astype(jnp.bfloat16)
        outgoing = stacked.reshape(seq_count * group_heads, 3, patches, patch_dev * HD)
        incoming = lax.all_to_all(outgoing, "seq", split_axis=0, concat_axis=3, tiled=True)
        incoming = incoming.reshape(3, patches, patch_len, HD)
        fresh_rows = jnp.concatenate([incoming[1], incoming[2]], axis=-1).reshape(
            total_len, 2 * HD
        )
        key_rows = jnp.where(use_fresh[:, :, None], fresh_rows[None], stale_rows[None])
        scores = (
            jnp.einsum(
                "pqe,pke->pqk", incoming[0], key_rows[..., :HD], preferred_element_type=jnp.float32
            )
            * scale_factor
        )
        scores = jnp.where(live_keys[None, None, :], scores, -jnp.inf)
        row_max = jnp.max(scores, axis=-1, keepdims=True)
        weights = jnp.exp(scores - row_max)
        row_sum = jnp.sum(weights, axis=-1, keepdims=True)
        combined = jnp.einsum(
            "pqk,pke->pqe",
            weights.astype(jnp.bfloat16),
            key_rows[..., HD:],
            preferred_element_type=jnp.float32,
        )
        attended = (combined / row_sum).astype(jnp.bfloat16)
        attended = attended.reshape(patches, seq_devices, patch_dev * HD)[None]
        returned = lax.all_to_all(attended, "seq", split_axis=2, concat_axis=0, tiled=True)
        returned = returned.reshape(seq_count, group_heads, patches, patch_dev, HD)
        update = scatter_cfg(
            jnp.einsum("sgpqe,dge->spqd", returned, out_full, preferred_element_type=jnp.float32),
            active,
        )
        result = (hidden.astype(jnp.float32) + gate_rows * update).astype(jnp.bfloat16)
        return result, fresh_rows

    first_out, first_cache = run(hidden_states, 0)
    received = from_behind(first_out, "section", 1)
    second_out, second_cache = run(received, 1)
    key_cache = jnp.where(section_id == 0, first_cache, second_cache)

    normed = row_norm(second_out.astype(jnp.float32))
    normed_out = (normed * (1.0 + out_modulation[1]) + out_modulation[0]).astype(jnp.bfloat16)
    predicted = jnp.einsum(
        "spqd,do->spqo", normed_out, proj_weight, preferred_element_type=jnp.float32
    )
    predicted_all = gather_cfg(predicted, 1)
    predicted_all = jnp.where(
        section_id == 0, from_behind(predicted_all, "section", 1), predicted_all
    )
    pair_rows = lax.dynamic_slice_in_dim(predicted_all, 2 * section_id, 2, 0)
    solver_row = solver_coef[0]
    guided = pair_rows[0] + solver_row[2] * (pair_rows[1] - pair_rows[0])
    new_latent = solver_row[0] * latent[0] + solver_row[1] * guided
    return (new_latent[None], key_cache[None, None, None])


def solution(mesh):
    return jax.shard_map(
        per_device,
        mesh=mesh,
        in_specs=(
            P("cfg", None, "seq", None),
            P("section", None, "seq", None),
            P("section", "cfg", "seq", None, None),
            P("section", None, None, "cfg"),
            P("section", "seq", "cfg"),
            P("section", None, None),
            P(),
            P(),
            P("section", None),
            P(),
            P(),
            P(None, None, None, "seq"),
        ),
        out_specs=(P("section", None, "seq", None), P("section", "cfg", "seq", None, None)),
        check_vma=False,
    )
```

```python
import math

import jax
import jax.numpy as jnp
from jax import lax
from jax.sharding import PartitionSpec as P

HD = 64
TEXT = 226


def from_behind(value, axis, steps):
    count = lax.axis_size(axis)
    pairs = [(source, (source + steps) % count) for source in range(count)]
    return lax.ppermute(value, axis, pairs)


def row_norm(values):
    centered = values - jnp.mean(values, axis=-1, keepdims=True)
    return centered * lax.rsqrt(jnp.mean(centered * centered, axis=-1, keepdims=True) + 1e-05)


def head_norm(values):
    centered = values - jnp.mean(values, axis=-1, keepdims=True)
    return centered * lax.rsqrt(jnp.mean(centered * centered, axis=-1, keepdims=True) + 1e-06)


def rope_angles(places, head_size):
    half_size = head_size // 2
    pairs_t = head_size // 8
    pairs_h = (half_size - pairs_t) // 2
    pair_index = jnp.arange(half_size)
    first_part = pair_index < pairs_t
    second_part = jnp.logical_and(pair_index >= pairs_t, pair_index < pairs_t + pairs_h)
    third_part = pair_index >= pairs_t + pairs_h
    local_index = jnp.where(
        first_part,
        pair_index,
        jnp.where(second_part, pair_index - pairs_t, pair_index - pairs_t - pairs_h),
    )
    axis_span = jnp.where(first_part, 2 * pairs_t, 2 * pairs_h)
    frequency = jnp.exp(
        -math.log(10000.0) * 2.0 * local_index.astype(jnp.float32) / axis_span.astype(jnp.float32)
    )
    angles = places[0][..., None] * first_part.astype(jnp.float32)
    angles = angles + places[1][..., None] * second_part.astype(jnp.float32)
    angles = angles + places[2][..., None] * third_part.astype(jnp.float32)
    return angles * frequency


def rotate(values, cos_table, sin_table):
    half_size = values.shape[-1] // 2
    first_half = values[..., :half_size]
    second_half = values[..., half_size:]
    return jnp.concatenate(
        [
            first_half * cos_table - second_half * sin_table,
            second_half * cos_table + first_half * sin_table,
        ],
        axis=-1,
    )


def shift_within(value, active, steps):
    count = lax.axis_size("cfg")
    pairs = [
        (active * count + source, active * count + (source + steps) % count)
        for source in range(count)
    ]
    return lax.ppermute(value, ("section", "cfg"), pairs)


def gather_cfg(values, active):
    count = lax.axis_size("cfg")
    here = lax.axis_index("cfg")
    slots = [values] + [shift_within(values, active, shift) for shift in range(1, count)]
    ordered = jnp.concatenate(slots[::-1], axis=0)
    return jnp.roll(ordered, here + 1, axis=0)


def scatter_cfg(partials, active):
    count = lax.axis_size("cfg")
    here = lax.axis_index("cfg")
    total = lax.dynamic_index_in_dim(partials, here, 0, keepdims=True)
    for shift in range(1, count):
        outgoing = lax.dynamic_index_in_dim(partials, (here + shift) % count, 0, keepdims=True)
        outgoing = outgoing.astype(jnp.bfloat16)
        total = total + shift_within(outgoing, active, shift).astype(jnp.float32)
    return total


def per_device(
    hidden_states,
    latent,
    stale_cache,
    qkv_weight,
    out_weight,
    modulation,
    out_modulation,
    proj_weight,
    solver_coef,
    video_len,
    text_len,
    positions,
):
    section_id = lax.axis_index("section")
    shard_id = lax.axis_index("seq")
    seq_devices = lax.axis_size("seq")
    cfg_devices = lax.axis_size("cfg")
    patches = hidden_states.shape[1]
    patch_dev = hidden_states.shape[2]
    width = hidden_states.shape[3]
    patch_len = patch_dev * seq_devices
    total_len = patch_len * patches
    group_heads = qkv_weight.shape[3] // HD
    seq_count = cfg_devices
    qkv_full = qkv_weight[0].reshape(width, 3 * group_heads * HD)

    def gather_out():
        return lax.all_gather(out_weight[0], "seq", axis=0, tiled=True).reshape(
            width, group_heads, HD
        )

    mod_rows = modulation[0]
    stale_rows = stale_cache[0, 0, 0]
    my_sequence = shard_id // group_heads
    row_ids = jnp.arange(total_len)
    text_limit = lax.dynamic_index_in_dim(text_len, my_sequence, keepdims=False)
    video_limit = lax.dynamic_index_in_dim(video_len, my_sequence // 2, keepdims=False)
    live_keys = jnp.where(row_ids < TEXT, row_ids < text_limit, row_ids - TEXT < video_limit)
    key_patch = row_ids // patch_len
    use_fresh = key_patch[None, :] <= jnp.arange(patches)[:, None]
    scale_factor = HD ** (-0.5)

    row_place = (
        jnp.arange(patches)[:, None] * patch_len
        + shard_id * patch_dev
        + jnp.arange(patch_dev)[None, :]
    )
    text_rows = (row_place < TEXT)[:, :, None]
    shift_rows = jnp.where(text_rows, mod_rows[3], mod_rows[0])
    scale_rows = jnp.where(text_rows, mod_rows[4], mod_rows[1])
    gate_rows = jnp.where(text_rows, mod_rows[5], mod_rows[2])
    angles = rope_angles(positions.astype(jnp.float32), HD)
    angles = jnp.where(text_rows[None], 0.0, angles)
    angles = jnp.repeat(angles, 2, axis=0)[:, None]
    cos_table = jnp.cos(angles)
    sin_table = jnp.sin(angles)

    def run(hidden, active, out_full):
        normed = row_norm(hidden.astype(jnp.float32))
        mixed_rows = (normed * (1.0 + scale_rows) + shift_rows).astype(jnp.bfloat16)
        mixed_rows = gather_cfg(mixed_rows, active)
        projected = jnp.dot(
            mixed_rows.reshape(-1, width), qkv_full, preferred_element_type=jnp.float32
        )
        projected = projected.reshape(seq_count, patches, patch_dev, 3, group_heads, HD)
        projected = projected.transpose(0, 4, 3, 1, 2, 5)
        queries = rotate(head_norm(projected[:, :, 0]), cos_table, sin_table)
        key_part = rotate(head_norm(projected[:, :, 1]), cos_table, sin_table)
        stacked = jnp.stack([queries, key_part, projected[:, :, 2]], axis=2).astype(jnp.bfloat16)
        outgoing = stacked.reshape(seq_count * group_heads, 3, patches, patch_dev * HD)
        incoming = lax.all_to_all(outgoing, "seq", split_axis=0, concat_axis=3, tiled=True)
        incoming = incoming.reshape(3, patches, patch_len, HD)
        fresh_rows = jnp.concatenate([incoming[1], incoming[2]], axis=-1).reshape(
            total_len, 2 * HD
        )
        key_rows = jnp.where(use_fresh[:, :, None], fresh_rows[None], stale_rows[None])
        scores = (
            jnp.einsum(
                "pqe,pke->pqk", incoming[0], key_rows[..., :HD], preferred_element_type=jnp.float32
            )
            * scale_factor
        )
        scores = jnp.where(live_keys[None, None, :], scores, -jnp.inf)
        row_max = jnp.max(scores, axis=-1, keepdims=True)
        weights = jnp.exp(scores - row_max)
        row_sum = jnp.sum(weights, axis=-1, keepdims=True)
        combined = jnp.einsum(
            "pqk,pke->pqe",
            weights.astype(jnp.bfloat16),
            key_rows[..., HD:],
            preferred_element_type=jnp.float32,
        )
        attended = (combined / row_sum).astype(jnp.bfloat16)
        attended = attended.reshape(patches, seq_devices, patch_dev * HD)[None]
        returned = lax.all_to_all(attended, "seq", split_axis=2, concat_axis=0, tiled=True)
        returned = returned.reshape(seq_count, group_heads, patches, patch_dev, HD)
        update = scatter_cfg(
            jnp.einsum("sgpqe,dge->spqd", returned, out_full, preferred_element_type=jnp.float32),
            active,
        )
        result = (hidden.astype(jnp.float32) + gate_rows * update).astype(jnp.bfloat16)
        return result, fresh_rows

    idle_cache = jnp.zeros((total_len, 2 * HD), jnp.bfloat16)

    def first_active(hidden):
        out_full = gather_out()
        return run(hidden, 0, out_full) + (out_full,)

    def first_idle(hidden):
        return hidden, idle_cache, gather_out()

    first_out, first_cache, out_full = lax.cond(
        section_id == 0, first_active, first_idle, hidden_states
    )
    received = from_behind(first_out, "section", 1)
    second_out, second_cache = lax.cond(
        section_id == 1,
        lambda hidden: run(hidden, 1, out_full),
        lambda hidden: (hidden, idle_cache),
        received,
    )
    key_cache = jnp.where(section_id == 0, first_cache, second_cache)

    normed = row_norm(second_out.astype(jnp.float32))
    normed_out = (normed * (1.0 + out_modulation[1]) + out_modulation[0]).astype(jnp.bfloat16)
    predicted = jnp.einsum(
        "spqd,do->spqo", normed_out, proj_weight, preferred_element_type=jnp.float32
    )
    predicted_all = gather_cfg(predicted, 1)
    predicted_all = jnp.where(
        section_id == 0, from_behind(predicted_all, "section", 1), predicted_all
    )
    pair_rows = lax.dynamic_slice_in_dim(predicted_all, 2 * section_id, 2, 0)
    solver_row = solver_coef[0]
    guided = pair_rows[0] + solver_row[2] * (pair_rows[1] - pair_rows[0])
    new_latent = solver_row[0] * latent[0] + solver_row[1] * guided
    return (new_latent[None], key_cache[None, None, None])


def solution(mesh):
    return jax.shard_map(
        per_device,
        mesh=mesh,
        in_specs=(
            P("cfg", None, "seq", None),
            P("section", None, "seq", None),
            P("section", "cfg", "seq", None, None),
            P("section", None, None, "cfg"),
            P("section", "seq", "cfg"),
            P("section", None, None),
            P(),
            P(),
            P("section", None),
            P(),
            P(),
            P(None, None, None, "seq"),
        ),
        out_specs=(P("section", None, "seq", None), P("section", "cfg", "seq", None, None)),
        check_vma=False,
    )
```

```python
import math

import jax
import jax.numpy as jnp
from jax import lax
from jax.sharding import PartitionSpec as P

HD = 64
TEXT = 226


def from_behind(value, axis, steps):
    count = lax.axis_size(axis)
    pairs = [(source, (source + steps) % count) for source in range(count)]
    return lax.ppermute(value, axis, pairs)


def row_norm(values):
    centered = values - jnp.mean(values, axis=-1, keepdims=True)
    return centered * lax.rsqrt(jnp.mean(centered * centered, axis=-1, keepdims=True) + 1e-05)


def head_norm(values):
    centered = values - jnp.mean(values, axis=-1, keepdims=True)
    return centered * lax.rsqrt(jnp.mean(centered * centered, axis=-1, keepdims=True) + 1e-06)


def rope_angles(places, head_size):
    half_size = head_size // 2
    pairs_t = head_size // 8
    pairs_h = (half_size - pairs_t) // 2
    pair_index = jnp.arange(half_size)
    first_part = pair_index < pairs_t
    second_part = jnp.logical_and(pair_index >= pairs_t, pair_index < pairs_t + pairs_h)
    third_part = pair_index >= pairs_t + pairs_h
    local_index = jnp.where(
        first_part,
        pair_index,
        jnp.where(second_part, pair_index - pairs_t, pair_index - pairs_t - pairs_h),
    )
    axis_span = jnp.where(first_part, 2 * pairs_t, 2 * pairs_h)
    frequency = jnp.exp(
        -math.log(10000.0) * 2.0 * local_index.astype(jnp.float32) / axis_span.astype(jnp.float32)
    )
    angles = places[0][..., None] * first_part.astype(jnp.float32)
    angles = angles + places[1][..., None] * second_part.astype(jnp.float32)
    angles = angles + places[2][..., None] * third_part.astype(jnp.float32)
    return angles * frequency


def rotate(values, cos_table, sin_table):
    half_size = values.shape[-1] // 2
    first_half = values[..., :half_size]
    second_half = values[..., half_size:]
    return jnp.concatenate(
        [
            first_half * cos_table - second_half * sin_table,
            second_half * cos_table + first_half * sin_table,
        ],
        axis=-1,
    )


def shift_within(value, active, steps):
    count = lax.axis_size("cfg")
    pairs = [
        (active * count + source, active * count + (source + steps) % count)
        for source in range(count)
    ]
    return lax.ppermute(value, ("section", "cfg"), pairs)


def gather_cfg(values, active):
    count = lax.axis_size("cfg")
    here = lax.axis_index("cfg")
    slots = [values] + [shift_within(values, active, shift) for shift in range(1, count)]
    ordered = jnp.concatenate(slots[::-1], axis=0)
    return jnp.roll(ordered, here + 1, axis=0)


def spread_across(values):
    count = lax.axis_size("cfg")
    here = lax.axis_index("cfg")
    slots = []
    for shift in range(count):
        pairs = [(source, count + (source + shift) % count) for source in range(count)]
        slots.append(lax.ppermute(values, ("section", "cfg"), pairs))
    ordered = jnp.concatenate(slots[::-1], axis=0)
    return jnp.roll(ordered, here + 1, axis=0)


def scatter_cfg(partials, active):
    count = lax.axis_size("cfg")
    here = lax.axis_index("cfg")
    total = lax.dynamic_index_in_dim(partials, here, 0, keepdims=True)
    for shift in range(1, count):
        outgoing = lax.dynamic_index_in_dim(partials, (here + shift) % count, 0, keepdims=True)
        outgoing = outgoing.astype(jnp.bfloat16)
        total = total + shift_within(outgoing, active, shift).astype(jnp.float32)
    return total


def per_device(
    hidden_states,
    latent,
    stale_cache,
    qkv_weight,
    out_weight,
    modulation,
    out_modulation,
    proj_weight,
    solver_coef,
    video_len,
    text_len,
    positions,
):
    section_id = lax.axis_index("section")
    shard_id = lax.axis_index("seq")
    seq_devices = lax.axis_size("seq")
    cfg_devices = lax.axis_size("cfg")
    patches = hidden_states.shape[1]
    patch_dev = hidden_states.shape[2]
    width = hidden_states.shape[3]
    patch_len = patch_dev * seq_devices
    total_len = patch_len * patches
    group_heads = qkv_weight.shape[3] // HD
    seq_count = cfg_devices
    qkv_full = qkv_weight[0].reshape(width, 3 * group_heads * HD)
    out_full = lax.all_gather(out_weight[0], "seq", axis=0, tiled=True).reshape(
        width, group_heads, HD
    )
    mod_rows = modulation[0]
    stale_rows = stale_cache[0, 0, 0]
    my_sequence = shard_id // group_heads
    row_ids = jnp.arange(total_len)
    text_limit = lax.dynamic_index_in_dim(text_len, my_sequence, keepdims=False)
    video_limit = lax.dynamic_index_in_dim(video_len, my_sequence // 2, keepdims=False)
    live_keys = jnp.where(row_ids < TEXT, row_ids < text_limit, row_ids - TEXT < video_limit)
    key_patch = row_ids // patch_len
    use_fresh = key_patch[None, :] <= jnp.arange(patches)[:, None]
    scale_factor = HD ** (-0.5)

    row_place = (
        jnp.arange(patches)[:, None] * patch_len
        + shard_id * patch_dev
        + jnp.arange(patch_dev)[None, :]
    )
    text_rows = (row_place < TEXT)[:, :, None]
    shift_rows = jnp.where(text_rows, mod_rows[3], mod_rows[0])
    scale_rows = jnp.where(text_rows, mod_rows[4], mod_rows[1])
    gate_rows = jnp.where(text_rows, mod_rows[5], mod_rows[2])
    angles = rope_angles(positions.astype(jnp.float32), HD)
    angles = jnp.where(text_rows[None], 0.0, angles)
    angles = jnp.repeat(angles, 2, axis=0)[:, None]
    cos_table = jnp.cos(angles)
    sin_table = jnp.sin(angles)

    def run(hidden, active, hidden_all=None):
        if hidden_all is None:
            normed = row_norm(hidden.astype(jnp.float32))
            mixed_rows = (normed * (1.0 + scale_rows) + shift_rows).astype(jnp.bfloat16)
            mixed_rows = gather_cfg(mixed_rows, active)
        else:
            normed = row_norm(hidden_all.astype(jnp.float32))
            mixed_rows = (normed * (1.0 + scale_rows) + shift_rows).astype(jnp.bfloat16)
        projected = jnp.dot(
            mixed_rows.reshape(-1, width), qkv_full, preferred_element_type=jnp.float32
        )
        projected = projected.reshape(seq_count, patches, patch_dev, 3, group_heads, HD)
        projected = projected.transpose(0, 4, 3, 1, 2, 5)
        queries = rotate(head_norm(projected[:, :, 0]), cos_table, sin_table)
        key_part = rotate(head_norm(projected[:, :, 1]), cos_table, sin_table)
        stacked = jnp.stack([queries, key_part, projected[:, :, 2]], axis=2).astype(jnp.bfloat16)
        outgoing = stacked.reshape(seq_count * group_heads, 3, patches, patch_dev * HD)
        incoming = lax.all_to_all(outgoing, "seq", split_axis=0, concat_axis=3, tiled=True)
        incoming = incoming.reshape(3, patches, patch_len, HD)
        fresh_rows = jnp.concatenate([incoming[1], incoming[2]], axis=-1).reshape(
            total_len, 2 * HD
        )
        key_rows = jnp.where(use_fresh[:, :, None], fresh_rows[None], stale_rows[None])
        scores = (
            jnp.einsum(
                "pqe,pke->pqk", incoming[0], key_rows[..., :HD], preferred_element_type=jnp.float32
            )
            * scale_factor
        )
        scores = jnp.where(live_keys[None, None, :], scores, -jnp.inf)
        row_max = jnp.max(scores, axis=-1, keepdims=True)
        weights = jnp.exp(scores - row_max)
        row_sum = jnp.sum(weights, axis=-1, keepdims=True)
        combined = jnp.einsum(
            "pqk,pke->pqe",
            weights.astype(jnp.bfloat16),
            key_rows[..., HD:],
            preferred_element_type=jnp.float32,
        )
        attended = (combined / row_sum).astype(jnp.bfloat16)
        attended = attended.reshape(patches, seq_devices, patch_dev * HD)[None]
        returned = lax.all_to_all(attended, "seq", split_axis=2, concat_axis=0, tiled=True)
        returned = returned.reshape(seq_count, group_heads, patches, patch_dev, HD)
        update = scatter_cfg(
            jnp.einsum("sgpqe,dge->spqd", returned, out_full, preferred_element_type=jnp.float32),
            active,
        )
        result = (hidden.astype(jnp.float32) + gate_rows * update).astype(jnp.bfloat16)
        return result, fresh_rows

    first_out, first_cache = run(hidden_states, 0)
    received_all = spread_across(first_out)
    received = lax.dynamic_index_in_dim(
        received_all, lax.axis_index("cfg"), 0, keepdims=True
    )
    second_out, second_cache = run(received, 1, received_all)
    key_cache = jnp.where(section_id == 0, first_cache, second_cache)

    normed = row_norm(second_out.astype(jnp.float32))
    normed_out = (normed * (1.0 + out_modulation[1]) + out_modulation[0]).astype(jnp.bfloat16)
    predicted = jnp.einsum(
        "spqd,do->spqo", normed_out, proj_weight, preferred_element_type=jnp.float32
    )
    predicted_all = gather_cfg(predicted, 1)
    predicted_all = jnp.where(
        section_id == 0, from_behind(predicted_all, "section", 1), predicted_all
    )
    pair_rows = lax.dynamic_slice_in_dim(predicted_all, 2 * section_id, 2, 0)
    solver_row = solver_coef[0]
    guided = pair_rows[0] + solver_row[2] * (pair_rows[1] - pair_rows[0])
    new_latent = solver_row[0] * latent[0] + solver_row[1] * guided
    return (new_latent[None], key_cache[None, None, None])


def solution(mesh):
    return jax.shard_map(
        per_device,
        mesh=mesh,
        in_specs=(
            P("cfg", None, "seq", None),
            P("section", None, "seq", None),
            P("section", "cfg", "seq", None, None),
            P("section", None, None, "cfg"),
            P("section", "seq", "cfg"),
            P("section", None, None),
            P(),
            P(),
            P("section", None),
            P(),
            P(),
            P(None, None, None, "seq"),
        ),
        out_specs=(P("section", None, "seq", None), P("section", "cfg", "seq", None, None)),
        check_vma=False,
    )
```

```python
import math

import jax
import jax.numpy as jnp
from jax import lax
from jax.experimental import pallas as pl
from jax.sharding import PartitionSpec as P

HD = 64
TEXT = 226


def from_behind(value, axis, steps):
    count = lax.axis_size(axis)
    pairs = [(source, (source + steps) % count) for source in range(count)]
    return lax.ppermute(value, axis, pairs)


def row_norm(values):
    centered = values - jnp.mean(values, axis=-1, keepdims=True)
    return centered * lax.rsqrt(jnp.mean(centered * centered, axis=-1, keepdims=True) + 1e-05)


def head_norm(values):
    centered = values - jnp.mean(values, axis=-1, keepdims=True)
    return centered * lax.rsqrt(jnp.mean(centered * centered, axis=-1, keepdims=True) + 1e-06)


def rope_angles(places, head_size):
    half_size = head_size // 2
    pairs_t = head_size // 8
    pairs_h = (half_size - pairs_t) // 2
    pair_index = jnp.arange(half_size)
    first_part = pair_index < pairs_t
    second_part = jnp.logical_and(pair_index >= pairs_t, pair_index < pairs_t + pairs_h)
    third_part = pair_index >= pairs_t + pairs_h
    local_index = jnp.where(
        first_part,
        pair_index,
        jnp.where(second_part, pair_index - pairs_t, pair_index - pairs_t - pairs_h),
    )
    axis_span = jnp.where(first_part, 2 * pairs_t, 2 * pairs_h)
    frequency = jnp.exp(
        -math.log(10000.0) * 2.0 * local_index.astype(jnp.float32) / axis_span.astype(jnp.float32)
    )
    angles = places[0][..., None] * first_part.astype(jnp.float32)
    angles = angles + places[1][..., None] * second_part.astype(jnp.float32)
    angles = angles + places[2][..., None] * third_part.astype(jnp.float32)
    return angles * frequency


def rotate(values, cos_table, sin_table):
    half_size = values.shape[-1] // 2
    first_half = values[..., :half_size]
    second_half = values[..., half_size:]
    return jnp.concatenate(
        [
            first_half * cos_table - second_half * sin_table,
            second_half * cos_table + first_half * sin_table,
        ],
        axis=-1,
    )


def shift_within(value, active, steps):
    count = lax.axis_size("cfg")
    pairs = [
        (active * count + source, active * count + (source + steps) % count)
        for source in range(count)
    ]
    return lax.ppermute(value, ("section", "cfg"), pairs)


def gather_cfg(values, active):
    count = lax.axis_size("cfg")
    here = lax.axis_index("cfg")
    slots = [values] + [shift_within(values, active, shift) for shift in range(1, count)]
    ordered = jnp.concatenate(slots[::-1], axis=0)
    return jnp.roll(ordered, here + 1, axis=0)


def scatter_cfg(partials, active):
    count = lax.axis_size("cfg")
    here = lax.axis_index("cfg")
    total = lax.dynamic_index_in_dim(partials, here, 0, keepdims=True)
    for shift in range(1, count):
        outgoing = lax.dynamic_index_in_dim(partials, (here + shift) % count, 0, keepdims=True)
        outgoing = outgoing.astype(jnp.bfloat16)
        total = total + shift_within(outgoing, active, shift).astype(jnp.float32)
    return total


def attend_kernel(query_ref, fresh_ref, stale_ref, live_ref, out_ref):
    patch_id = pl.program_id(0)
    patch_len = query_ref.shape[1]
    total_len = fresh_ref.shape[0]
    key_patch = lax.broadcasted_iota(jnp.int32, (total_len, 1), 0) // patch_len
    use_fresh = key_patch <= patch_id
    key_rows = jnp.where(use_fresh, fresh_ref[:, :HD], stale_ref[:, :HD])
    value_rows = jnp.where(use_fresh, fresh_ref[:, HD:], stale_ref[:, HD:])
    scores = lax.dot_general(
        query_ref[0],
        key_rows,
        (((1,), (1,)), ((), ())),
        preferred_element_type=jnp.float32,
    ) * (HD ** (-0.5))
    scores = jnp.where(live_ref[...] > 0, scores, -jnp.inf)
    row_max = jnp.max(scores, axis=1, keepdims=True)
    weights = jnp.exp(scores - row_max)
    row_sum = jnp.sum(weights, axis=1, keepdims=True)
    combined = jnp.dot(
        weights.astype(jnp.bfloat16), value_rows, preferred_element_type=jnp.float32
    )
    out_ref[0] = (combined / row_sum).astype(out_ref.dtype)


def attend(queries, fresh_rows, stale_rows, live_flags):
    patches, patch_len, head_size = queries.shape
    total_len, pair_size = fresh_rows.shape
    return pl.pallas_call(
        attend_kernel,
        grid=(patches,),
        in_specs=[
            pl.BlockSpec((1, patch_len, head_size), lambda p: (p, 0, 0)),
            pl.BlockSpec((total_len, pair_size), lambda p: (0, 0)),
            pl.BlockSpec((total_len, pair_size), lambda p: (0, 0)),
            pl.BlockSpec((1, total_len), lambda p: (0, 0)),
        ],
        out_specs=pl.BlockSpec((1, patch_len, head_size), lambda p: (p, 0, 0)),
        out_shape=jax.ShapeDtypeStruct(queries.shape, jnp.bfloat16),
    )(queries, fresh_rows, stale_rows, live_flags)


def per_device(
    hidden_states,
    latent,
    stale_cache,
    qkv_weight,
    out_weight,
    modulation,
    out_modulation,
    proj_weight,
    solver_coef,
    video_len,
    text_len,
    positions,
):
    section_id = lax.axis_index("section")
    shard_id = lax.axis_index("seq")
    seq_devices = lax.axis_size("seq")
    cfg_devices = lax.axis_size("cfg")
    patches = hidden_states.shape[1]
    patch_dev = hidden_states.shape[2]
    width = hidden_states.shape[3]
    patch_len = patch_dev * seq_devices
    total_len = patch_len * patches
    group_heads = qkv_weight.shape[3] // HD
    seq_count = cfg_devices
    qkv_full = qkv_weight[0].reshape(width, 3 * group_heads * HD)
    out_full = lax.all_gather(out_weight[0], "seq", axis=0, tiled=True).reshape(
        width, group_heads, HD
    )
    mod_rows = modulation[0]
    stale_rows = stale_cache[0, 0, 0]
    my_sequence = shard_id // group_heads
    row_ids = jnp.arange(total_len)
    text_limit = lax.dynamic_index_in_dim(text_len, my_sequence, keepdims=False)
    video_limit = lax.dynamic_index_in_dim(video_len, my_sequence // 2, keepdims=False)
    live_keys = jnp.where(row_ids < TEXT, row_ids < text_limit, row_ids - TEXT < video_limit)
    live_flags = live_keys.astype(jnp.int32)[None, :]
    scale_factor = HD ** (-0.5)

    row_place = (
        jnp.arange(patches)[:, None] * patch_len
        + shard_id * patch_dev
        + jnp.arange(patch_dev)[None, :]
    )
    text_rows = (row_place < TEXT)[:, :, None]
    shift_rows = jnp.where(text_rows, mod_rows[3], mod_rows[0])
    scale_rows = jnp.where(text_rows, mod_rows[4], mod_rows[1])
    gate_rows = jnp.where(text_rows, mod_rows[5], mod_rows[2])
    angles = rope_angles(positions.astype(jnp.float32), HD)
    angles = jnp.where(text_rows[None], 0.0, angles)
    angles = jnp.repeat(angles, 2, axis=0)[:, None]
    cos_table = jnp.cos(angles)
    sin_table = jnp.sin(angles)

    def run(hidden, active):
        normed = row_norm(hidden.astype(jnp.float32))
        mixed_rows = (normed * (1.0 + scale_rows) + shift_rows).astype(jnp.bfloat16)
        mixed_rows = gather_cfg(mixed_rows, active)
        projected = jnp.dot(
            mixed_rows.reshape(-1, width), qkv_full, preferred_element_type=jnp.float32
        )
        projected = projected.reshape(seq_count, patches, patch_dev, 3, group_heads, HD)
        projected = projected.transpose(0, 4, 3, 1, 2, 5)
        queries = rotate(head_norm(projected[:, :, 0]), cos_table, sin_table)
        key_part = rotate(head_norm(projected[:, :, 1]), cos_table, sin_table)
        stacked = jnp.stack([queries, key_part, projected[:, :, 2]], axis=2).astype(jnp.bfloat16)
        outgoing = stacked.reshape(seq_count * group_heads, 3, patches, patch_dev * HD)
        incoming = lax.all_to_all(outgoing, "seq", split_axis=0, concat_axis=3, tiled=True)
        incoming = incoming.reshape(3, patches, patch_len, HD)
        fresh_rows = jnp.concatenate([incoming[1], incoming[2]], axis=-1).reshape(
            total_len, 2 * HD
        )
        attended = attend(incoming[0], fresh_rows, stale_rows, live_flags)
        attended = attended.reshape(patches, seq_devices, patch_dev * HD)[None]
        returned = lax.all_to_all(attended, "seq", split_axis=2, concat_axis=0, tiled=True)
        returned = returned.reshape(seq_count, group_heads, patches, patch_dev, HD)
        update = scatter_cfg(
            jnp.einsum("sgpqe,dge->spqd", returned, out_full, preferred_element_type=jnp.float32),
            active,
        )
        result = (hidden.astype(jnp.float32) + gate_rows * update).astype(jnp.bfloat16)
        return result, fresh_rows

    first_out, first_cache = run(hidden_states, 0)
    received = from_behind(first_out, "section", 1)
    second_out, second_cache = run(received, 1)
    key_cache = jnp.where(section_id == 0, first_cache, second_cache)

    normed = row_norm(second_out.astype(jnp.float32))
    normed_out = (normed * (1.0 + out_modulation[1]) + out_modulation[0]).astype(jnp.bfloat16)
    predicted = jnp.einsum(
        "spqd,do->spqo", normed_out, proj_weight, preferred_element_type=jnp.float32
    )
    predicted_all = gather_cfg(predicted, 1)
    predicted_all = jnp.where(
        section_id == 0, from_behind(predicted_all, "section", 1), predicted_all
    )
    pair_rows = lax.dynamic_slice_in_dim(predicted_all, 2 * section_id, 2, 0)
    solver_row = solver_coef[0]
    guided = pair_rows[0] + solver_row[2] * (pair_rows[1] - pair_rows[0])
    new_latent = solver_row[0] * latent[0] + solver_row[1] * guided
    return (new_latent[None], key_cache[None, None, None])


def solution(mesh):
    return jax.shard_map(
        per_device,
        mesh=mesh,
        in_specs=(
            P("cfg", None, "seq", None),
            P("section", None, "seq", None),
            P("section", "cfg", "seq", None, None),
            P("section", None, None, "cfg"),
            P("section", "seq", "cfg"),
            P("section", None, None),
            P(),
            P(),
            P("section", None),
            P(),
            P(),
            P(None, None, None, "seq"),
        ),
        out_specs=(P("section", None, "seq", None), P("section", "cfg", "seq", None, None)),
        check_vma=False,
    )
```

```python
import math

import jax
import jax.numpy as jnp
from jax import lax
from jax.experimental import pallas as pl
from jax.sharding import PartitionSpec as P

HD = 64
TEXT = 226


def from_behind(value, axis, steps):
    count = lax.axis_size(axis)
    pairs = [(source, (source + steps) % count) for source in range(count)]
    return lax.ppermute(value, axis, pairs)


def row_norm(values):
    centered = values - jnp.mean(values, axis=-1, keepdims=True)
    return centered * lax.rsqrt(jnp.mean(centered * centered, axis=-1, keepdims=True) + 1e-05)


def head_norm(values):
    centered = values - jnp.mean(values, axis=-1, keepdims=True)
    return centered * lax.rsqrt(jnp.mean(centered * centered, axis=-1, keepdims=True) + 1e-06)


def rope_angles(places, head_size):
    half_size = head_size // 2
    pairs_t = head_size // 8
    pairs_h = (half_size - pairs_t) // 2
    pair_index = jnp.arange(half_size)
    first_part = pair_index < pairs_t
    second_part = jnp.logical_and(pair_index >= pairs_t, pair_index < pairs_t + pairs_h)
    third_part = pair_index >= pairs_t + pairs_h
    local_index = jnp.where(
        first_part,
        pair_index,
        jnp.where(second_part, pair_index - pairs_t, pair_index - pairs_t - pairs_h),
    )
    axis_span = jnp.where(first_part, 2 * pairs_t, 2 * pairs_h)
    frequency = jnp.exp(
        -math.log(10000.0) * 2.0 * local_index.astype(jnp.float32) / axis_span.astype(jnp.float32)
    )
    angles = places[0][..., None] * first_part.astype(jnp.float32)
    angles = angles + places[1][..., None] * second_part.astype(jnp.float32)
    angles = angles + places[2][..., None] * third_part.astype(jnp.float32)
    return angles * frequency


def rotate(values, cos_table, sin_table):
    half_size = values.shape[-1] // 2
    first_half = values[..., :half_size]
    second_half = values[..., half_size:]
    return jnp.concatenate(
        [
            first_half * cos_table - second_half * sin_table,
            second_half * cos_table + first_half * sin_table,
        ],
        axis=-1,
    )


def shift_within(value, active, steps):
    count = lax.axis_size("cfg")
    pairs = [
        (active * count + source, active * count + (source + steps) % count)
        for source in range(count)
    ]
    return lax.ppermute(value, ("section", "cfg"), pairs)


def gather_cfg(values, active):
    count = lax.axis_size("cfg")
    here = lax.axis_index("cfg")
    slots = [values] + [shift_within(values, active, shift) for shift in range(1, count)]
    ordered = jnp.concatenate(slots[::-1], axis=0)
    return jnp.roll(ordered, here + 1, axis=0)


def scatter_cfg(partials, active):
    count = lax.axis_size("cfg")
    here = lax.axis_index("cfg")
    total = lax.dynamic_index_in_dim(partials, here, 0, keepdims=True)
    for shift in range(1, count):
        outgoing = lax.dynamic_index_in_dim(partials, (here + shift) % count, 0, keepdims=True)
        outgoing = outgoing.astype(jnp.bfloat16)
        total = total + shift_within(outgoing, active, shift).astype(jnp.float32)
    return total


def attend_kernel(query_ref, fresh_ref, stale_ref, live_ref, out_ref):
    patch_id = pl.program_id(0)
    patch_len = query_ref.shape[1]
    total_len = fresh_ref.shape[0]
    key_patch = lax.broadcasted_iota(jnp.int32, (total_len, 1), 0) // patch_len
    use_fresh = key_patch <= patch_id
    key_rows = jnp.where(use_fresh, fresh_ref[:, :HD], stale_ref[:, :HD])
    value_rows = jnp.where(use_fresh, fresh_ref[:, HD:], stale_ref[:, HD:])
    scores = lax.dot_general(
        query_ref[0] * jnp.asarray(HD ** (-0.5), query_ref.dtype),
        key_rows,
        (((1,), (1,)), ((), ())),
        preferred_element_type=jnp.float32,
    )
    scores = jnp.where(live_ref[...] > 0, scores, -jnp.inf)
    row_max = jnp.max(scores, axis=1, keepdims=True)
    weights = jnp.exp(scores - row_max)
    row_sum = jnp.sum(weights, axis=1, keepdims=True)
    combined = jnp.dot(
        weights.astype(jnp.bfloat16), value_rows, preferred_element_type=jnp.float32
    )
    out_ref[0] = (combined / row_sum).astype(out_ref.dtype)


def attend(queries, fresh_rows, stale_rows, live_flags):
    patches, patch_len, head_size = queries.shape
    total_len, pair_size = fresh_rows.shape
    return pl.pallas_call(
        attend_kernel,
        grid=(patches,),
        in_specs=[
            pl.BlockSpec((1, patch_len, head_size), lambda p: (p, 0, 0)),
            pl.BlockSpec((total_len, pair_size), lambda p: (0, 0)),
            pl.BlockSpec((total_len, pair_size), lambda p: (0, 0)),
            pl.BlockSpec((1, total_len), lambda p: (0, 0)),
        ],
        out_specs=pl.BlockSpec((1, patch_len, head_size), lambda p: (p, 0, 0)),
        out_shape=jax.ShapeDtypeStruct(queries.shape, jnp.bfloat16),
    )(queries, fresh_rows, stale_rows, live_flags)


def per_device(
    hidden_states,
    latent,
    stale_cache,
    qkv_weight,
    out_weight,
    modulation,
    out_modulation,
    proj_weight,
    solver_coef,
    video_len,
    text_len,
    positions,
):
    section_id = lax.axis_index("section")
    shard_id = lax.axis_index("seq")
    seq_devices = lax.axis_size("seq")
    cfg_devices = lax.axis_size("cfg")
    patches = hidden_states.shape[1]
    patch_dev = hidden_states.shape[2]
    width = hidden_states.shape[3]
    patch_len = patch_dev * seq_devices
    total_len = patch_len * patches
    group_heads = qkv_weight.shape[3] // HD
    seq_count = cfg_devices
    qkv_full = qkv_weight[0].reshape(width, 3 * group_heads * HD)
    out_full = lax.all_gather(out_weight[0], "seq", axis=0, tiled=True).reshape(
        width, group_heads, HD
    )
    mod_rows = modulation[0]
    stale_rows = stale_cache[0, 0, 0]
    my_sequence = shard_id // group_heads
    row_ids = jnp.arange(total_len)
    text_limit = lax.dynamic_index_in_dim(text_len, my_sequence, keepdims=False)
    video_limit = lax.dynamic_index_in_dim(video_len, my_sequence // 2, keepdims=False)
    live_keys = jnp.where(row_ids < TEXT, row_ids < text_limit, row_ids - TEXT < video_limit)
    live_flags = live_keys.astype(jnp.int32)[None, :]
    scale_factor = HD ** (-0.5)

    row_place = (
        jnp.arange(patches)[:, None] * patch_len
        + shard_id * patch_dev
        + jnp.arange(patch_dev)[None, :]
    )
    text_rows = (row_place < TEXT)[:, :, None]
    shift_rows = jnp.where(text_rows, mod_rows[3], mod_rows[0])
    scale_rows = jnp.where(text_rows, mod_rows[4], mod_rows[1])
    gate_rows = jnp.where(text_rows, mod_rows[5], mod_rows[2])
    angles = rope_angles(positions.astype(jnp.float32), HD)
    angles = jnp.where(text_rows[None], 0.0, angles)
    angles = jnp.repeat(angles, 2, axis=0)[:, None]
    cos_table = jnp.cos(angles)
    sin_table = jnp.sin(angles)

    def run(hidden, active):
        normed = row_norm(hidden.astype(jnp.float32))
        mixed_rows = (normed * (1.0 + scale_rows) + shift_rows).astype(jnp.bfloat16)
        mixed_rows = gather_cfg(mixed_rows, active)
        projected = jnp.dot(
            mixed_rows.reshape(-1, width), qkv_full, preferred_element_type=jnp.float32
        )
        projected = projected.reshape(seq_count, patches, patch_dev, 3, group_heads, HD)
        projected = projected.transpose(0, 4, 3, 1, 2, 5)
        queries = rotate(head_norm(projected[:, :, 0]), cos_table, sin_table)
        key_part = rotate(head_norm(projected[:, :, 1]), cos_table, sin_table)
        stacked = jnp.stack([queries, key_part, projected[:, :, 2]], axis=2).astype(jnp.bfloat16)
        outgoing = stacked.reshape(seq_count * group_heads, 3, patches, patch_dev * HD)
        incoming = lax.all_to_all(outgoing, "seq", split_axis=0, concat_axis=3, tiled=True)
        incoming = incoming.reshape(3, patches, patch_len, HD)
        fresh_rows = jnp.concatenate([incoming[1], incoming[2]], axis=-1).reshape(
            total_len, 2 * HD
        )
        attended = attend(incoming[0], fresh_rows, stale_rows, live_flags)
        attended = attended.reshape(patches, seq_devices, patch_dev * HD)[None]
        returned = lax.all_to_all(attended, "seq", split_axis=2, concat_axis=0, tiled=True)
        returned = returned.reshape(seq_count, group_heads, patches, patch_dev, HD)
        update = scatter_cfg(
            jnp.einsum("sgpqe,dge->spqd", returned, out_full, preferred_element_type=jnp.float32),
            active,
        )
        result = (hidden.astype(jnp.float32) + gate_rows * update).astype(jnp.bfloat16)
        return result, fresh_rows

    first_out, first_cache = run(hidden_states, 0)
    received = from_behind(first_out, "section", 1)
    second_out, second_cache = run(received, 1)
    key_cache = jnp.where(section_id == 0, first_cache, second_cache)

    normed = row_norm(second_out.astype(jnp.float32))
    normed_out = (normed * (1.0 + out_modulation[1]) + out_modulation[0]).astype(jnp.bfloat16)
    predicted = jnp.einsum(
        "spqd,do->spqo", normed_out, proj_weight, preferred_element_type=jnp.float32
    )
    count = cfg_devices
    here = lax.axis_index("cfg")
    slots = []
    for step in range(count):
        pairs = [(count, step), (count + 1, (step + 1) % count)]
        if step < count - 1:
            pairs += [(count + 2, count + (3 + step) % count), (count + 3, count + step)]
        slots.append(lax.ppermute(predicted, ("section", "cfg"), pairs))
    slots = jnp.concatenate(slots, axis=0)
    first_table = jnp.array([1, 2, 0, 0], jnp.int32)
    second_table = jnp.array([0, 1, 2, 0], jnp.int32)
    first_at = jnp.where(section_id == 0, here, first_table[here])
    second_at = jnp.where(section_id == 0, (here + count - 1) % count, second_table[here])
    first_rows = lax.dynamic_index_in_dim(slots, first_at, 0, keepdims=False)
    second_rows = lax.dynamic_index_in_dim(slots, second_at, 0, keepdims=False)
    first_rows = jnp.where((section_id == 1) & (here == 2), predicted[0], first_rows)
    second_rows = jnp.where((section_id == 1) & (here == 3), predicted[0], second_rows)
    pair_rows = jnp.stack([first_rows, second_rows], axis=0)
    solver_row = solver_coef[0]
    guided = pair_rows[0] + solver_row[2] * (pair_rows[1] - pair_rows[0])
    new_latent = solver_row[0] * latent[0] + solver_row[1] * guided
    return (new_latent[None], key_cache[None, None, None])


def solution(mesh):
    return jax.shard_map(
        per_device,
        mesh=mesh,
        in_specs=(
            P("cfg", None, "seq", None),
            P("section", None, "seq", None),
            P("section", "cfg", "seq", None, None),
            P("section", None, None, "cfg"),
            P("section", "seq", "cfg"),
            P("section", None, None),
            P(),
            P(),
            P("section", None),
            P(),
            P(),
            P(None, None, None, "seq"),
        ),
        out_specs=(P("section", None, "seq", None), P("section", "cfg", "seq", None, None)),
        check_vma=False,
    )
```

```python
import math

import jax
import jax.numpy as jnp
from jax import lax
from jax.experimental import pallas as pl
from jax.sharding import PartitionSpec as P

HD = 64
TEXT = 226


def from_behind(value, axis, steps):
    count = lax.axis_size(axis)
    pairs = [(source, (source + steps) % count) for source in range(count)]
    return lax.ppermute(value, axis, pairs)


def row_norm(values):
    centered = values - jnp.mean(values, axis=-1, keepdims=True)
    return centered * lax.rsqrt(jnp.mean(centered * centered, axis=-1, keepdims=True) + 1e-05)


def head_norm(values):
    centered = values - jnp.mean(values, axis=-1, keepdims=True)
    return centered * lax.rsqrt(jnp.mean(centered * centered, axis=-1, keepdims=True) + 1e-06)


def rope_angles(places, head_size):
    half_size = head_size // 2
    pairs_t = head_size // 8
    pairs_h = (half_size - pairs_t) // 2
    pair_index = jnp.arange(half_size)
    first_part = pair_index < pairs_t
    second_part = jnp.logical_and(pair_index >= pairs_t, pair_index < pairs_t + pairs_h)
    third_part = pair_index >= pairs_t + pairs_h
    local_index = jnp.where(
        first_part,
        pair_index,
        jnp.where(second_part, pair_index - pairs_t, pair_index - pairs_t - pairs_h),
    )
    axis_span = jnp.where(first_part, 2 * pairs_t, 2 * pairs_h)
    frequency = jnp.exp(
        -math.log(10000.0) * 2.0 * local_index.astype(jnp.float32) / axis_span.astype(jnp.float32)
    )
    angles = places[0][..., None] * first_part.astype(jnp.float32)
    angles = angles + places[1][..., None] * second_part.astype(jnp.float32)
    angles = angles + places[2][..., None] * third_part.astype(jnp.float32)
    return angles * frequency


def rotate(values, cos_table, sin_table):
    half_size = values.shape[-1] // 2
    first_half = values[..., :half_size]
    second_half = values[..., half_size:]
    return jnp.concatenate(
        [
            first_half * cos_table - second_half * sin_table,
            second_half * cos_table + first_half * sin_table,
        ],
        axis=-1,
    )


def shift_within(value, active, steps):
    count = lax.axis_size("cfg")
    pairs = [
        (active * count + source, active * count + (source + steps) % count)
        for source in range(count)
    ]
    return lax.ppermute(value, ("section", "cfg"), pairs)


def gather_cfg(values, active):
    count = lax.axis_size("cfg")
    here = lax.axis_index("cfg")
    slots = [values] + [shift_within(values, active, shift) for shift in range(1, count)]
    ordered = jnp.concatenate(slots[::-1], axis=0)
    return jnp.roll(ordered, here + 1, axis=0)


def scatter_cfg(partials, active):
    count = lax.axis_size("cfg")
    here = lax.axis_index("cfg")
    total = lax.dynamic_index_in_dim(partials, here, 0, keepdims=True)
    for shift in range(1, count):
        outgoing = lax.dynamic_index_in_dim(partials, (here + shift) % count, 0, keepdims=True)
        outgoing = outgoing.astype(jnp.bfloat16)
        total = total + shift_within(outgoing, active, shift).astype(jnp.float32)
    return total


def attend_kernel(query_ref, fresh_ref, stale_ref, live_ref, out_ref):
    patch_id = pl.program_id(0)
    patch_len = query_ref.shape[1]
    total_len = fresh_ref.shape[0]
    key_patch = lax.broadcasted_iota(jnp.int32, (total_len, 1), 0) // patch_len
    use_fresh = key_patch <= patch_id
    key_rows = jnp.where(use_fresh, fresh_ref[:, :HD], stale_ref[:, :HD])
    value_rows = jnp.where(use_fresh, fresh_ref[:, HD:], stale_ref[:, HD:])
    scores = lax.dot_general(
        query_ref[0] * jnp.asarray(HD ** (-0.5), query_ref.dtype),
        key_rows,
        (((1,), (1,)), ((), ())),
        preferred_element_type=jnp.float32,
    )
    scores = jnp.where(live_ref[...] > 0, scores, -jnp.inf)
    row_max = jnp.max(scores, axis=1, keepdims=True)
    weights = jnp.exp(scores - row_max)
    row_sum = jnp.sum(weights, axis=1, keepdims=True)
    combined = jnp.dot(
        weights.astype(jnp.bfloat16), value_rows, preferred_element_type=jnp.float32
    )
    out_ref[0] = (combined / row_sum).astype(out_ref.dtype)


def attend(queries, fresh_rows, stale_rows, live_flags):
    patches, patch_len, head_size = queries.shape
    total_len, pair_size = fresh_rows.shape
    return pl.pallas_call(
        attend_kernel,
        grid=(patches,),
        in_specs=[
            pl.BlockSpec((1, patch_len, head_size), lambda p: (p, 0, 0)),
            pl.BlockSpec((total_len, pair_size), lambda p: (0, 0)),
            pl.BlockSpec((total_len, pair_size), lambda p: (0, 0)),
            pl.BlockSpec((1, total_len), lambda p: (0, 0)),
        ],
        out_specs=pl.BlockSpec((1, patch_len, head_size), lambda p: (p, 0, 0)),
        out_shape=jax.ShapeDtypeStruct(queries.shape, jnp.bfloat16),
    )(queries, fresh_rows, stale_rows, live_flags)


def out_project_kernel(att_ref, weight_ref, out_ref):
    heads = att_ref.shape[1]
    head_size = att_ref.shape[3]
    total = jnp.zeros(out_ref.shape[1:], jnp.float32)
    for head in range(heads):
        total = total + lax.dot_general(
            att_ref[0, head],
            weight_ref[:, head * head_size : (head + 1) * head_size],
            (((1,), (1,)), ((), ())),
            preferred_element_type=jnp.float32,
        )
    out_ref[0] = total


def out_project(attended, weight):
    seqs, heads, rows, head_size = attended.shape
    width = weight.shape[0]
    return pl.pallas_call(
        out_project_kernel,
        grid=(seqs,),
        in_specs=[
            pl.BlockSpec((1, heads, rows, head_size), lambda s: (s, 0, 0, 0)),
            pl.BlockSpec((width, heads * head_size), lambda s: (0, 0)),
        ],
        out_specs=pl.BlockSpec((1, rows, width), lambda s: (s, 0, 0)),
        out_shape=jax.ShapeDtypeStruct((seqs, rows, width), jnp.float32),
    )(attended, weight)


def per_device(
    hidden_states,
    latent,
    stale_cache,
    qkv_weight,
    out_weight,
    modulation,
    out_modulation,
    proj_weight,
    solver_coef,
    video_len,
    text_len,
    positions,
):
    section_id = lax.axis_index("section")
    shard_id = lax.axis_index("seq")
    seq_devices = lax.axis_size("seq")
    cfg_devices = lax.axis_size("cfg")
    patches = hidden_states.shape[1]
    patch_dev = hidden_states.shape[2]
    width = hidden_states.shape[3]
    patch_len = patch_dev * seq_devices
    total_len = patch_len * patches
    group_heads = qkv_weight.shape[3] // HD
    seq_count = cfg_devices
    qkv_full = qkv_weight[0].reshape(width, 3 * group_heads * HD)
    out_full = lax.all_gather(out_weight[0], "seq", axis=0, tiled=True)
    mod_rows = modulation[0]
    stale_rows = stale_cache[0, 0, 0]
    my_sequence = shard_id // group_heads
    row_ids = jnp.arange(total_len)
    text_limit = lax.dynamic_index_in_dim(text_len, my_sequence, keepdims=False)
    video_limit = lax.dynamic_index_in_dim(video_len, my_sequence // 2, keepdims=False)
    live_keys = jnp.where(row_ids < TEXT, row_ids < text_limit, row_ids - TEXT < video_limit)
    live_flags = live_keys.astype(jnp.int32)[None, :]
    scale_factor = HD ** (-0.5)

    row_place = (
        jnp.arange(patches)[:, None] * patch_len
        + shard_id * patch_dev
        + jnp.arange(patch_dev)[None, :]
    )
    text_rows = (row_place < TEXT)[:, :, None]
    shift_rows = jnp.where(text_rows, mod_rows[3], mod_rows[0])
    scale_rows = jnp.where(text_rows, mod_rows[4], mod_rows[1])
    gate_rows = jnp.where(text_rows, mod_rows[5], mod_rows[2])
    angles = rope_angles(positions.astype(jnp.float32), HD)
    angles = jnp.where(text_rows[None], 0.0, angles)
    angles = jnp.repeat(angles, 2, axis=0)[:, None]
    cos_table = jnp.cos(angles)
    sin_table = jnp.sin(angles)

    def run(hidden, active):
        normed = row_norm(hidden.astype(jnp.float32))
        mixed_rows = (normed * (1.0 + scale_rows) + shift_rows).astype(jnp.bfloat16)
        mixed_rows = gather_cfg(mixed_rows, active)
        projected = jnp.dot(
            mixed_rows.reshape(-1, width), qkv_full, preferred_element_type=jnp.float32
        )
        projected = projected.reshape(seq_count, patches, patch_dev, 3, group_heads, HD)
        projected = projected.transpose(0, 4, 3, 1, 2, 5)
        queries = rotate(head_norm(projected[:, :, 0]), cos_table, sin_table)
        key_part = rotate(head_norm(projected[:, :, 1]), cos_table, sin_table)
        stacked = jnp.stack([queries, key_part, projected[:, :, 2]], axis=2).astype(jnp.bfloat16)
        outgoing = stacked.reshape(seq_count * group_heads, 3, patches, patch_dev * HD)
        incoming = lax.all_to_all(outgoing, "seq", split_axis=0, concat_axis=3, tiled=True)
        incoming = incoming.reshape(3, patches, patch_len, HD)
        fresh_rows = jnp.concatenate([incoming[1], incoming[2]], axis=-1).reshape(
            total_len, 2 * HD
        )
        attended = attend(incoming[0], fresh_rows, stale_rows, live_flags)
        attended = attended.reshape(patches, seq_devices, patch_dev * HD)[None]
        returned = lax.all_to_all(attended, "seq", split_axis=2, concat_axis=0, tiled=True)
        returned = returned.reshape(seq_count, group_heads, patches * patch_dev, HD)
        update = out_project(returned, out_full).reshape(seq_count, patches, patch_dev, width)
        update = scatter_cfg(update, active)
        result = (hidden.astype(jnp.float32) + gate_rows * update).astype(jnp.bfloat16)
        return result, fresh_rows

    first_out, first_cache = run(hidden_states, 0)
    received = from_behind(first_out, "section", 1)
    second_out, second_cache = run(received, 1)
    key_cache = jnp.where(section_id == 0, first_cache, second_cache)

    normed = row_norm(second_out.astype(jnp.float32))
    normed_out = (normed * (1.0 + out_modulation[1]) + out_modulation[0]).astype(jnp.bfloat16)
    predicted = jnp.einsum(
        "spqd,do->spqo", normed_out, proj_weight, preferred_element_type=jnp.float32
    )
    count = cfg_devices
    here = lax.axis_index("cfg")
    slots = []
    for step in range(count):
        pairs = [(count, step), (count + 1, (step + 1) % count)]
        if step < count - 1:
            pairs += [(count + 2, count + (3 + step) % count), (count + 3, count + step)]
        slots.append(lax.ppermute(predicted, ("section", "cfg"), pairs))
    slots = jnp.concatenate(slots, axis=0)
    first_table = jnp.array([1, 2, 0, 0], jnp.int32)
    second_table = jnp.array([0, 1, 2, 0], jnp.int32)
    first_at = jnp.where(section_id == 0, here, first_table[here])
    second_at = jnp.where(section_id == 0, (here + count - 1) % count, second_table[here])
    first_rows = lax.dynamic_index_in_dim(slots, first_at, 0, keepdims=False)
    second_rows = lax.dynamic_index_in_dim(slots, second_at, 0, keepdims=False)
    first_rows = jnp.where((section_id == 1) & (here == 2), predicted[0], first_rows)
    second_rows = jnp.where((section_id == 1) & (here == 3), predicted[0], second_rows)
    pair_rows = jnp.stack([first_rows, second_rows], axis=0)
    solver_row = solver_coef[0]
    guided = pair_rows[0] + solver_row[2] * (pair_rows[1] - pair_rows[0])
    new_latent = solver_row[0] * latent[0] + solver_row[1] * guided
    return (new_latent[None], key_cache[None, None, None])


def solution(mesh):
    return jax.shard_map(
        per_device,
        mesh=mesh,
        in_specs=(
            P("cfg", None, "seq", None),
            P("section", None, "seq", None),
            P("section", "cfg", "seq", None, None),
            P("section", None, None, "cfg"),
            P("section", "seq", "cfg"),
            P("section", None, None),
            P(),
            P(),
            P("section", None),
            P(),
            P(),
            P(None, None, None, "seq"),
        ),
        out_specs=(P("section", None, "seq", None), P("section", "cfg", "seq", None, None)),
        check_vma=False,
    )
```

```python
import math

import jax
import jax.numpy as jnp
from jax import lax
from jax.experimental import pallas as pl
from jax.sharding import PartitionSpec as P

HD = 64
TEXT = 226


def from_behind(value, axis, steps):
    count = lax.axis_size(axis)
    pairs = [(source, (source + steps) % count) for source in range(count)]
    return lax.ppermute(value, axis, pairs)


def row_norm(values):
    centered = values - jnp.mean(values, axis=-1, keepdims=True)
    return centered * lax.rsqrt(jnp.mean(centered * centered, axis=-1, keepdims=True) + 1e-05)


def head_norm(values):
    centered = values - jnp.mean(values, axis=-1, keepdims=True)
    return centered * lax.rsqrt(jnp.mean(centered * centered, axis=-1, keepdims=True) + 1e-06)


def rope_angles(places, head_size):
    half_size = head_size // 2
    pairs_t = head_size // 8
    pairs_h = (half_size - pairs_t) // 2
    pair_index = jnp.arange(half_size)
    first_part = pair_index < pairs_t
    second_part = jnp.logical_and(pair_index >= pairs_t, pair_index < pairs_t + pairs_h)
    third_part = pair_index >= pairs_t + pairs_h
    local_index = jnp.where(
        first_part,
        pair_index,
        jnp.where(second_part, pair_index - pairs_t, pair_index - pairs_t - pairs_h),
    )
    axis_span = jnp.where(first_part, 2 * pairs_t, 2 * pairs_h)
    frequency = jnp.exp(
        -math.log(10000.0) * 2.0 * local_index.astype(jnp.float32) / axis_span.astype(jnp.float32)
    )
    angles = places[0][..., None] * first_part.astype(jnp.float32)
    angles = angles + places[1][..., None] * second_part.astype(jnp.float32)
    angles = angles + places[2][..., None] * third_part.astype(jnp.float32)
    return angles * frequency


def rotate(values, cos_table, sin_table):
    half_size = values.shape[-1] // 2
    first_half = values[..., :half_size]
    second_half = values[..., half_size:]
    return jnp.concatenate(
        [
            first_half * cos_table - second_half * sin_table,
            second_half * cos_table + first_half * sin_table,
        ],
        axis=-1,
    )


def shift_within(value, active, steps):
    count = lax.axis_size("cfg")
    pairs = [
        (active * count + source, active * count + (source + steps) % count)
        for source in range(count)
    ]
    return lax.ppermute(value, ("section", "cfg"), pairs)


def gather_cfg(values, active):
    count = lax.axis_size("cfg")
    here = lax.axis_index("cfg")
    slots = [values] + [shift_within(values, active, shift) for shift in range(1, count)]
    ordered = jnp.concatenate(slots[::-1], axis=0)
    return jnp.roll(ordered, here + 1, axis=0)


def scatter_cfg(partials, active):
    count = lax.axis_size("cfg")
    here = lax.axis_index("cfg")
    total = lax.dynamic_index_in_dim(partials, here, 0, keepdims=True)
    for shift in range(1, count):
        outgoing = lax.dynamic_index_in_dim(partials, (here + shift) % count, 0, keepdims=True)
        outgoing = outgoing.astype(jnp.bfloat16)
        total = total + shift_within(outgoing, active, shift).astype(jnp.float32)
    return total


def mix_kernel(rows_ref, flag_ref, mod_ref, out_ref):
    values = rows_ref[...].astype(jnp.float32)
    centered = values - jnp.mean(values, axis=-1, keepdims=True)
    normed = centered * lax.rsqrt(jnp.mean(centered * centered, axis=-1, keepdims=True) + 1e-05)
    text = flag_ref[...] > 0
    shift = jnp.where(text, mod_ref[2:3, :], mod_ref[0:1, :])
    scale = jnp.where(text, mod_ref[3:4, :], mod_ref[1:2, :])
    out_ref[...] = (normed * (1.0 + scale) + shift).astype(out_ref.dtype)


def mix(rows, flags, mods):
    shape = rows.shape
    rows = rows.reshape(-1, shape[-1])
    count, width = rows.shape
    flags = jnp.broadcast_to(flags.reshape(1, -1, 1), (count // flags.size, flags.size, 1))
    flags = flags.reshape(count, 1)
    out = pl.pallas_call(
        mix_kernel,
        grid=(1,),
        in_specs=[
            pl.BlockSpec((count, width), lambda i: (0, 0)),
            pl.BlockSpec((count, 1), lambda i: (0, 0)),
            pl.BlockSpec(mods.shape, lambda i: (0, 0)),
        ],
        out_specs=pl.BlockSpec((count, width), lambda i: (0, 0)),
        out_shape=jax.ShapeDtypeStruct((count, width), jnp.bfloat16),
    )(rows, flags, mods)
    return out.reshape(shape)


def attend_kernel(query_ref, fresh_ref, stale_ref, live_ref, out_ref):
    patch_id = pl.program_id(0)
    patch_len = query_ref.shape[1]
    total_len = fresh_ref.shape[0]
    key_patch = lax.broadcasted_iota(jnp.int32, (total_len, 1), 0) // patch_len
    use_fresh = key_patch <= patch_id
    key_rows = jnp.where(use_fresh, fresh_ref[:, :HD], stale_ref[:, :HD])
    value_rows = jnp.where(use_fresh, fresh_ref[:, HD:], stale_ref[:, HD:])
    scores = lax.dot_general(
        query_ref[0] * jnp.asarray(HD ** (-0.5), query_ref.dtype),
        key_rows,
        (((1,), (1,)), ((), ())),
        preferred_element_type=jnp.float32,
    )
    scores = jnp.where(live_ref[...] > 0, scores, -jnp.inf)
    row_max = jnp.max(scores, axis=1, keepdims=True)
    weights = jnp.exp(scores - row_max)
    row_sum = jnp.sum(weights, axis=1, keepdims=True)
    combined = jnp.dot(
        weights.astype(jnp.bfloat16), value_rows, preferred_element_type=jnp.float32
    )
    out_ref[0] = (combined / row_sum).astype(out_ref.dtype)


def attend(queries, fresh_rows, stale_rows, live_flags):
    patches, patch_len, head_size = queries.shape
    total_len, pair_size = fresh_rows.shape
    return pl.pallas_call(
        attend_kernel,
        grid=(patches,),
        in_specs=[
            pl.BlockSpec((1, patch_len, head_size), lambda p: (p, 0, 0)),
            pl.BlockSpec((total_len, pair_size), lambda p: (0, 0)),
            pl.BlockSpec((total_len, pair_size), lambda p: (0, 0)),
            pl.BlockSpec((1, total_len), lambda p: (0, 0)),
        ],
        out_specs=pl.BlockSpec((1, patch_len, head_size), lambda p: (p, 0, 0)),
        out_shape=jax.ShapeDtypeStruct(queries.shape, jnp.bfloat16),
    )(queries, fresh_rows, stale_rows, live_flags)


def per_device(
    hidden_states,
    latent,
    stale_cache,
    qkv_weight,
    out_weight,
    modulation,
    out_modulation,
    proj_weight,
    solver_coef,
    video_len,
    text_len,
    positions,
):
    section_id = lax.axis_index("section")
    shard_id = lax.axis_index("seq")
    seq_devices = lax.axis_size("seq")
    cfg_devices = lax.axis_size("cfg")
    patches = hidden_states.shape[1]
    patch_dev = hidden_states.shape[2]
    width = hidden_states.shape[3]
    patch_len = patch_dev * seq_devices
    total_len = patch_len * patches
    group_heads = qkv_weight.shape[3] // HD
    seq_count = cfg_devices
    qkv_full = qkv_weight[0].reshape(width, 3 * group_heads * HD)
    out_full = lax.all_gather(out_weight[0], "seq", axis=0, tiled=True).reshape(
        width, group_heads, HD
    )
    mod_rows = modulation[0]
    stale_rows = stale_cache[0, 0, 0]
    my_sequence = shard_id // group_heads
    row_ids = jnp.arange(total_len)
    text_limit = lax.dynamic_index_in_dim(text_len, my_sequence, keepdims=False)
    video_limit = lax.dynamic_index_in_dim(video_len, my_sequence // 2, keepdims=False)
    live_keys = jnp.where(row_ids < TEXT, row_ids < text_limit, row_ids - TEXT < video_limit)
    live_flags = live_keys.astype(jnp.int32)[None, :]
    scale_factor = HD ** (-0.5)

    row_place = (
        jnp.arange(patches)[:, None] * patch_len
        + shard_id * patch_dev
        + jnp.arange(patch_dev)[None, :]
    )
    text_rows = (row_place < TEXT)[:, :, None]
    text_flags = text_rows.astype(jnp.float32)
    layer_mods = jnp.stack([mod_rows[0], mod_rows[1], mod_rows[3], mod_rows[4]], axis=0)
    out_mods = jnp.stack([out_modulation[0], out_modulation[1]] * 2, axis=0)
    shift_rows = jnp.where(text_rows, mod_rows[3], mod_rows[0])
    scale_rows = jnp.where(text_rows, mod_rows[4], mod_rows[1])
    gate_rows = jnp.where(text_rows, mod_rows[5], mod_rows[2])
    angles = rope_angles(positions.astype(jnp.float32), HD)
    angles = jnp.where(text_rows[None], 0.0, angles)
    angles = jnp.repeat(angles, 2, axis=0)[:, None]
    cos_table = jnp.cos(angles)
    sin_table = jnp.sin(angles)

    def run(hidden, active):
        mixed_rows = mix(hidden, text_flags, layer_mods)
        mixed_rows = gather_cfg(mixed_rows, active)
        projected = jnp.dot(
            mixed_rows.reshape(-1, width), qkv_full, preferred_element_type=jnp.float32
        )
        projected = projected.reshape(seq_count, patches, patch_dev, 3, group_heads, HD)
        projected = projected.transpose(0, 4, 3, 1, 2, 5)
        queries = rotate(head_norm(projected[:, :, 0]), cos_table, sin_table)
        key_part = rotate(head_norm(projected[:, :, 1]), cos_table, sin_table)
        stacked = jnp.stack([queries, key_part, projected[:, :, 2]], axis=2).astype(jnp.bfloat16)
        outgoing = stacked.reshape(seq_count * group_heads, 3, patches, patch_dev * HD)
        incoming = lax.all_to_all(outgoing, "seq", split_axis=0, concat_axis=3, tiled=True)
        incoming = incoming.reshape(3, patches, patch_len, HD)
        fresh_rows = jnp.concatenate([incoming[1], incoming[2]], axis=-1).reshape(
            total_len, 2 * HD
        )
        attended = attend(incoming[0], fresh_rows, stale_rows, live_flags)
        attended = attended.reshape(patches, seq_devices, patch_dev * HD)[None]
        returned = lax.all_to_all(attended, "seq", split_axis=2, concat_axis=0, tiled=True)
        returned = returned.reshape(seq_count, group_heads, patches, patch_dev, HD)
        update = scatter_cfg(
            jnp.einsum("sgpqe,dge->spqd", returned, out_full, preferred_element_type=jnp.float32),
            active,
        )
        result = (hidden.astype(jnp.float32) + gate_rows * update).astype(jnp.bfloat16)
        return result, fresh_rows

    first_out, first_cache = run(hidden_states, 0)
    received = from_behind(first_out, "section", 1)
    second_out, second_cache = run(received, 1)
    key_cache = jnp.where(section_id == 0, first_cache, second_cache)

    normed_out = mix(second_out, text_flags, out_mods)
    predicted = jnp.einsum(
        "spqd,do->spqo", normed_out, proj_weight, preferred_element_type=jnp.float32
    )
    count = cfg_devices
    here = lax.axis_index("cfg")
    slots = []
    for step in range(count):
        pairs = [(count, step), (count + 1, (step + 1) % count)]
        if step < count - 1:
            pairs += [(count + 2, count + (3 + step) % count), (count + 3, count + step)]
        slots.append(lax.ppermute(predicted, ("section", "cfg"), pairs))
    slots = jnp.concatenate(slots, axis=0)
    first_table = jnp.array([1, 2, 0, 0], jnp.int32)
    second_table = jnp.array([0, 1, 2, 0], jnp.int32)
    first_at = jnp.where(section_id == 0, here, first_table[here])
    second_at = jnp.where(section_id == 0, (here + count - 1) % count, second_table[here])
    first_rows = lax.dynamic_index_in_dim(slots, first_at, 0, keepdims=False)
    second_rows = lax.dynamic_index_in_dim(slots, second_at, 0, keepdims=False)
    first_rows = jnp.where((section_id == 1) & (here == 2), predicted[0], first_rows)
    second_rows = jnp.where((section_id == 1) & (here == 3), predicted[0], second_rows)
    pair_rows = jnp.stack([first_rows, second_rows], axis=0)
    solver_row = solver_coef[0]
    guided = pair_rows[0] + solver_row[2] * (pair_rows[1] - pair_rows[0])
    new_latent = solver_row[0] * latent[0] + solver_row[1] * guided
    return (new_latent[None], key_cache[None, None, None])


def solution(mesh):
    return jax.shard_map(
        per_device,
        mesh=mesh,
        in_specs=(
            P("cfg", None, "seq", None),
            P("section", None, "seq", None),
            P("section", "cfg", "seq", None, None),
            P("section", None, None, "cfg"),
            P("section", "seq", "cfg"),
            P("section", None, None),
            P(),
            P(),
            P("section", None),
            P(),
            P(),
            P(None, None, None, "seq"),
        ),
        out_specs=(P("section", None, "seq", None), P("section", "cfg", "seq", None, None)),
        check_vma=False,
    )
```

```python
import math

import jax
import jax.numpy as jnp
from jax import lax
from jax.experimental import pallas as pl
from jax.sharding import PartitionSpec as P

HD = 64
TEXT = 226


def from_behind(value, axis, steps):
    count = lax.axis_size(axis)
    pairs = [(source, (source + steps) % count) for source in range(count)]
    return lax.ppermute(value, axis, pairs)


def row_norm(values):
    centered = values - jnp.mean(values, axis=-1, keepdims=True)
    return centered * lax.rsqrt(jnp.mean(centered * centered, axis=-1, keepdims=True) + 1e-05)


def head_norm(values):
    centered = values - jnp.mean(values, axis=-1, keepdims=True)
    return centered * lax.rsqrt(jnp.mean(centered * centered, axis=-1, keepdims=True) + 1e-06)


def rope_angles(places, head_size):
    half_size = head_size // 2
    pairs_t = head_size // 8
    pairs_h = (half_size - pairs_t) // 2
    pair_index = jnp.arange(half_size)
    first_part = pair_index < pairs_t
    second_part = jnp.logical_and(pair_index >= pairs_t, pair_index < pairs_t + pairs_h)
    third_part = pair_index >= pairs_t + pairs_h
    local_index = jnp.where(
        first_part,
        pair_index,
        jnp.where(second_part, pair_index - pairs_t, pair_index - pairs_t - pairs_h),
    )
    axis_span = jnp.where(first_part, 2 * pairs_t, 2 * pairs_h)
    frequency = jnp.exp(
        -math.log(10000.0) * 2.0 * local_index.astype(jnp.float32) / axis_span.astype(jnp.float32)
    )
    angles = places[0][..., None] * first_part.astype(jnp.float32)
    angles = angles + places[1][..., None] * second_part.astype(jnp.float32)
    angles = angles + places[2][..., None] * third_part.astype(jnp.float32)
    return angles * frequency


def rotate(values, cos_table, sin_table):
    half_size = values.shape[-1] // 2
    first_half = values[..., :half_size]
    second_half = values[..., half_size:]
    return jnp.concatenate(
        [
            first_half * cos_table - second_half * sin_table,
            second_half * cos_table + first_half * sin_table,
        ],
        axis=-1,
    )


def shift_within(value, active, steps):
    count = lax.axis_size("cfg")
    pairs = [
        (active * count + source, active * count + (source + steps) % count)
        for source in range(count)
    ]
    return lax.ppermute(value, ("section", "cfg"), pairs)


def gather_cfg(values, active):
    count = lax.axis_size("cfg")
    here = lax.axis_index("cfg")
    slots = [values] + [shift_within(values, active, shift) for shift in range(1, count)]
    ordered = jnp.concatenate(slots[::-1], axis=0)
    return jnp.roll(ordered, here + 1, axis=0)


def scatter_cfg(partials, active):
    count = lax.axis_size("cfg")
    here = lax.axis_index("cfg")
    total = lax.dynamic_index_in_dim(partials, here, 0, keepdims=True)
    for shift in range(1, count):
        outgoing = lax.dynamic_index_in_dim(partials, (here + shift) % count, 0, keepdims=True)
        outgoing = outgoing.astype(jnp.bfloat16)
        total = total + shift_within(outgoing, active, shift).astype(jnp.float32)
    return total


def attend_kernel(query_ref, fresh_ref, stale_ref, live_ref, out_ref):
    patch_id = pl.program_id(0) // 2
    patch_len = 2 * query_ref.shape[1]
    total_len = fresh_ref.shape[0]
    key_patch = lax.broadcasted_iota(jnp.int32, (total_len, 1), 0) // patch_len
    use_fresh = key_patch <= patch_id
    key_rows = jnp.where(use_fresh, fresh_ref[:, :HD], stale_ref[:, :HD])
    value_rows = jnp.where(use_fresh, fresh_ref[:, HD:], stale_ref[:, HD:])
    scores = lax.dot_general(
        query_ref[0] * jnp.asarray(HD ** (-0.5), query_ref.dtype),
        key_rows,
        (((1,), (1,)), ((), ())),
        preferred_element_type=jnp.float32,
    )
    scores = jnp.where(live_ref[...] > 0, scores, -jnp.inf)
    row_max = jnp.max(scores, axis=1, keepdims=True)
    weights = jnp.exp(scores - row_max)
    row_sum = jnp.sum(weights, axis=1, keepdims=True)
    combined = jnp.dot(
        weights.astype(jnp.bfloat16), value_rows, preferred_element_type=jnp.float32
    )
    out_ref[0] = (combined / row_sum).astype(out_ref.dtype)


def attend(queries, fresh_rows, stale_rows, live_flags):
    patches, patch_len, head_size = queries.shape
    total_len, pair_size = fresh_rows.shape
    return pl.pallas_call(
        attend_kernel,
        grid=(2 * patches,),
        in_specs=[
            pl.BlockSpec((1, patch_len // 2, head_size), lambda p: (p // 2, p % 2, 0)),
            pl.BlockSpec((total_len, pair_size), lambda p: (0, 0)),
            pl.BlockSpec((total_len, pair_size), lambda p: (0, 0)),
            pl.BlockSpec((1, total_len), lambda p: (0, 0)),
        ],
        out_specs=pl.BlockSpec((1, patch_len // 2, head_size), lambda p: (p // 2, p % 2, 0)),
        out_shape=jax.ShapeDtypeStruct(queries.shape, jnp.bfloat16),
    )(queries, fresh_rows, stale_rows, live_flags)


def per_device(
    hidden_states,
    latent,
    stale_cache,
    qkv_weight,
    out_weight,
    modulation,
    out_modulation,
    proj_weight,
    solver_coef,
    video_len,
    text_len,
    positions,
):
    section_id = lax.axis_index("section")
    shard_id = lax.axis_index("seq")
    seq_devices = lax.axis_size("seq")
    cfg_devices = lax.axis_size("cfg")
    patches = hidden_states.shape[1]
    patch_dev = hidden_states.shape[2]
    width = hidden_states.shape[3]
    patch_len = patch_dev * seq_devices
    total_len = patch_len * patches
    group_heads = qkv_weight.shape[3] // HD
    seq_count = cfg_devices
    qkv_full = qkv_weight[0].reshape(width, 3 * group_heads * HD)
    out_full = lax.all_gather(out_weight[0], "seq", axis=0, tiled=True).reshape(
        width, group_heads, HD
    )
    mod_rows = modulation[0]
    stale_rows = stale_cache[0, 0, 0]
    my_sequence = shard_id // group_heads
    row_ids = jnp.arange(total_len)
    text_limit = lax.dynamic_index_in_dim(text_len, my_sequence, keepdims=False)
    video_limit = lax.dynamic_index_in_dim(video_len, my_sequence // 2, keepdims=False)
    live_keys = jnp.where(row_ids < TEXT, row_ids < text_limit, row_ids - TEXT < video_limit)
    live_flags = live_keys.astype(jnp.int32)[None, :]
    scale_factor = HD ** (-0.5)

    row_place = (
        jnp.arange(patches)[:, None] * patch_len
        + shard_id * patch_dev
        + jnp.arange(patch_dev)[None, :]
    )
    text_rows = (row_place < TEXT)[:, :, None]
    shift_rows = jnp.where(text_rows, mod_rows[3], mod_rows[0])
    scale_rows = jnp.where(text_rows, mod_rows[4], mod_rows[1])
    gate_rows = jnp.where(text_rows, mod_rows[5], mod_rows[2])
    angles = rope_angles(positions.astype(jnp.float32), HD)
    angles = jnp.where(text_rows[None], 0.0, angles)
    angles = jnp.repeat(angles, 2, axis=0)[:, None]
    cos_table = jnp.cos(angles)
    sin_table = jnp.sin(angles)

    def run(hidden, active):
        normed = row_norm(hidden.astype(jnp.float32))
        mixed_rows = (normed * (1.0 + scale_rows) + shift_rows).astype(jnp.bfloat16)
        mixed_rows = gather_cfg(mixed_rows, active)
        projected = jnp.dot(
            mixed_rows.reshape(-1, width), qkv_full, preferred_element_type=jnp.float32
        )
        projected = projected.reshape(seq_count, patches, patch_dev, 3, group_heads, HD)
        projected = projected.transpose(0, 4, 3, 1, 2, 5)
        queries = rotate(head_norm(projected[:, :, 0]), cos_table, sin_table)
        key_part = rotate(head_norm(projected[:, :, 1]), cos_table, sin_table)
        stacked = jnp.stack([queries, key_part, projected[:, :, 2]], axis=2).astype(jnp.bfloat16)
        outgoing = stacked.reshape(seq_count * group_heads, 3, patches, patch_dev * HD)
        incoming = lax.all_to_all(outgoing, "seq", split_axis=0, concat_axis=3, tiled=True)
        incoming = incoming.reshape(3, patches, patch_len, HD)
        fresh_rows = jnp.concatenate([incoming[1], incoming[2]], axis=-1).reshape(
            total_len, 2 * HD
        )
        attended = attend(incoming[0], fresh_rows, stale_rows, live_flags)
        attended = attended.reshape(patches, seq_devices, patch_dev * HD)[None]
        returned = lax.all_to_all(attended, "seq", split_axis=2, concat_axis=0, tiled=True)
        returned = returned.reshape(seq_count, group_heads, patches, patch_dev, HD)
        update = scatter_cfg(
            jnp.einsum("sgpqe,dge->spqd", returned, out_full, preferred_element_type=jnp.float32),
            active,
        )
        result = (hidden.astype(jnp.float32) + gate_rows * update).astype(jnp.bfloat16)
        return result, fresh_rows

    first_out, first_cache = run(hidden_states, 0)
    received = from_behind(first_out, "section", 1)
    second_out, second_cache = run(received, 1)
    key_cache = jnp.where(section_id == 0, first_cache, second_cache)

    normed = row_norm(second_out.astype(jnp.float32))
    normed_out = (normed * (1.0 + out_modulation[1]) + out_modulation[0]).astype(jnp.bfloat16)
    predicted = jnp.einsum(
        "spqd,do->spqo", normed_out, proj_weight, preferred_element_type=jnp.float32
    )
    count = cfg_devices
    here = lax.axis_index("cfg")
    slots = []
    for step in range(count):
        pairs = [(count, step), (count + 1, (step + 1) % count)]
        if step < count - 1:
            pairs += [(count + 2, count + (3 + step) % count), (count + 3, count + step)]
        slots.append(lax.ppermute(predicted, ("section", "cfg"), pairs))
    slots = jnp.concatenate(slots, axis=0)
    first_table = jnp.array([1, 2, 0, 0], jnp.int32)
    second_table = jnp.array([0, 1, 2, 0], jnp.int32)
    first_at = jnp.where(section_id == 0, here, first_table[here])
    second_at = jnp.where(section_id == 0, (here + count - 1) % count, second_table[here])
    first_rows = lax.dynamic_index_in_dim(slots, first_at, 0, keepdims=False)
    second_rows = lax.dynamic_index_in_dim(slots, second_at, 0, keepdims=False)
    first_rows = jnp.where((section_id == 1) & (here == 2), predicted[0], first_rows)
    second_rows = jnp.where((section_id == 1) & (here == 3), predicted[0], second_rows)
    pair_rows = jnp.stack([first_rows, second_rows], axis=0)
    solver_row = solver_coef[0]
    guided = pair_rows[0] + solver_row[2] * (pair_rows[1] - pair_rows[0])
    new_latent = solver_row[0] * latent[0] + solver_row[1] * guided
    return (new_latent[None], key_cache[None, None, None])


def solution(mesh):
    return jax.shard_map(
        per_device,
        mesh=mesh,
        in_specs=(
            P("cfg", None, "seq", None),
            P("section", None, "seq", None),
            P("section", "cfg", "seq", None, None),
            P("section", None, None, "cfg"),
            P("section", "seq", "cfg"),
            P("section", None, None),
            P(),
            P(),
            P("section", None),
            P(),
            P(),
            P(None, None, None, "seq"),
        ),
        out_specs=(P("section", None, "seq", None), P("section", "cfg", "seq", None, None)),
        check_vma=False,
    )
```

```python
import math

import jax
import jax.numpy as jnp
from jax import lax
from jax.experimental import pallas as pl
from jax.sharding import PartitionSpec as P

HD = 64
TEXT = 226


def from_behind(value, axis, steps):
    count = lax.axis_size(axis)
    pairs = [(source, (source + steps) % count) for source in range(count)]
    return lax.ppermute(value, axis, pairs)


def row_norm(values):
    centered = values - jnp.mean(values, axis=-1, keepdims=True)
    return centered * lax.rsqrt(jnp.mean(centered * centered, axis=-1, keepdims=True) + 1e-05)


def head_norm(values):
    centered = values - jnp.mean(values, axis=-1, keepdims=True)
    return centered * lax.rsqrt(jnp.mean(centered * centered, axis=-1, keepdims=True) + 1e-06)


def rope_angles(places, head_size):
    half_size = head_size // 2
    pairs_t = head_size // 8
    pairs_h = (half_size - pairs_t) // 2
    pair_index = jnp.arange(half_size)
    first_part = pair_index < pairs_t
    second_part = jnp.logical_and(pair_index >= pairs_t, pair_index < pairs_t + pairs_h)
    third_part = pair_index >= pairs_t + pairs_h
    local_index = jnp.where(
        first_part,
        pair_index,
        jnp.where(second_part, pair_index - pairs_t, pair_index - pairs_t - pairs_h),
    )
    axis_span = jnp.where(first_part, 2 * pairs_t, 2 * pairs_h)
    frequency = jnp.exp(
        -math.log(10000.0) * 2.0 * local_index.astype(jnp.float32) / axis_span.astype(jnp.float32)
    )
    angles = places[0][..., None] * first_part.astype(jnp.float32)
    angles = angles + places[1][..., None] * second_part.astype(jnp.float32)
    angles = angles + places[2][..., None] * third_part.astype(jnp.float32)
    return angles * frequency


def rotate(values, cos_table, sin_table):
    half_size = values.shape[-1] // 2
    first_half = values[..., :half_size]
    second_half = values[..., half_size:]
    return jnp.concatenate(
        [
            first_half * cos_table - second_half * sin_table,
            second_half * cos_table + first_half * sin_table,
        ],
        axis=-1,
    )


def shift_within(value, active, steps):
    count = lax.axis_size("cfg")
    pairs = [
        (active * count + source, active * count + (source + steps) % count)
        for source in range(count)
    ]
    return lax.ppermute(value, ("section", "cfg"), pairs)


def gather_cfg(values, active):
    count = lax.axis_size("cfg")
    here = lax.axis_index("cfg")
    slots = [values] + [shift_within(values, active, shift) for shift in range(1, count)]
    ordered = jnp.concatenate(slots[::-1], axis=0)
    return jnp.roll(ordered, here + 1, axis=0)


def scatter_cfg(partials, active):
    count = lax.axis_size("cfg")
    here = lax.axis_index("cfg")
    total = lax.dynamic_index_in_dim(partials, here, 0, keepdims=True)
    for shift in range(1, count):
        outgoing = lax.dynamic_index_in_dim(partials, (here + shift) % count, 0, keepdims=True)
        outgoing = outgoing.astype(jnp.bfloat16)
        total = total + shift_within(outgoing, active, shift).astype(jnp.float32)
    return total


def attend_kernel(query_ref, fresh_ref, stale_ref, live_ref, out_ref):
    patch_id = pl.program_id(0) // 4
    patch_len = 4 * query_ref.shape[1]
    total_len = fresh_ref.shape[0]
    key_patch = lax.broadcasted_iota(jnp.int32, (total_len, 1), 0) // patch_len
    use_fresh = key_patch <= patch_id
    key_rows = jnp.where(use_fresh, fresh_ref[:, :HD], stale_ref[:, :HD])
    value_rows = jnp.where(use_fresh, fresh_ref[:, HD:], stale_ref[:, HD:])
    scores = lax.dot_general(
        query_ref[0] * jnp.asarray(HD ** (-0.5), query_ref.dtype),
        key_rows,
        (((1,), (1,)), ((), ())),
        preferred_element_type=jnp.float32,
    )
    scores = jnp.where(live_ref[...] > 0, scores, -jnp.inf)
    row_max = jnp.max(scores, axis=1, keepdims=True)
    weights = jnp.exp(scores - row_max)
    row_sum = jnp.sum(weights, axis=1, keepdims=True)
    combined = jnp.dot(
        weights.astype(jnp.bfloat16), value_rows, preferred_element_type=jnp.float32
    )
    out_ref[0] = (combined / row_sum).astype(out_ref.dtype)


def attend(queries, fresh_rows, stale_rows, live_flags):
    patches, patch_len, head_size = queries.shape
    total_len, pair_size = fresh_rows.shape
    return pl.pallas_call(
        attend_kernel,
        grid=(4 * patches,),
        in_specs=[
            pl.BlockSpec((1, patch_len // 4, head_size), lambda p: (p // 4, p % 4, 0)),
            pl.BlockSpec((total_len, pair_size), lambda p: (0, 0)),
            pl.BlockSpec((total_len, pair_size), lambda p: (0, 0)),
            pl.BlockSpec((1, total_len), lambda p: (0, 0)),
        ],
        out_specs=pl.BlockSpec((1, patch_len // 4, head_size), lambda p: (p // 4, p % 4, 0)),
        out_shape=jax.ShapeDtypeStruct(queries.shape, jnp.bfloat16),
    )(queries, fresh_rows, stale_rows, live_flags)


def per_device(
    hidden_states,
    latent,
    stale_cache,
    qkv_weight,
    out_weight,
    modulation,
    out_modulation,
    proj_weight,
    solver_coef,
    video_len,
    text_len,
    positions,
):
    section_id = lax.axis_index("section")
    shard_id = lax.axis_index("seq")
    seq_devices = lax.axis_size("seq")
    cfg_devices = lax.axis_size("cfg")
    patches = hidden_states.shape[1]
    patch_dev = hidden_states.shape[2]
    width = hidden_states.shape[3]
    patch_len = patch_dev * seq_devices
    total_len = patch_len * patches
    group_heads = qkv_weight.shape[3] // HD
    seq_count = cfg_devices
    qkv_full = qkv_weight[0].reshape(width, 3 * group_heads * HD)
    out_full = lax.all_gather(out_weight[0], "seq", axis=0, tiled=True).reshape(
        width, group_heads, HD
    )
    mod_rows = modulation[0]
    stale_rows = stale_cache[0, 0, 0]
    my_sequence = shard_id // group_heads
    row_ids = jnp.arange(total_len)
    text_limit = lax.dynamic_index_in_dim(text_len, my_sequence, keepdims=False)
    video_limit = lax.dynamic_index_in_dim(video_len, my_sequence // 2, keepdims=False)
    live_keys = jnp.where(row_ids < TEXT, row_ids < text_limit, row_ids - TEXT < video_limit)
    live_flags = live_keys.astype(jnp.int32)[None, :]
    scale_factor = HD ** (-0.5)

    row_place = (
        jnp.arange(patches)[:, None] * patch_len
        + shard_id * patch_dev
        + jnp.arange(patch_dev)[None, :]
    )
    text_rows = (row_place < TEXT)[:, :, None]
    shift_rows = jnp.where(text_rows, mod_rows[3], mod_rows[0])
    scale_rows = jnp.where(text_rows, mod_rows[4], mod_rows[1])
    gate_rows = jnp.where(text_rows, mod_rows[5], mod_rows[2])
    angles = rope_angles(positions.astype(jnp.float32), HD)
    angles = jnp.where(text_rows[None], 0.0, angles)
    angles = jnp.repeat(angles, 2, axis=0)[:, None]
    cos_table = jnp.cos(angles)
    sin_table = jnp.sin(angles)

    def run(hidden, active):
        normed = row_norm(hidden.astype(jnp.float32))
        mixed_rows = (normed * (1.0 + scale_rows) + shift_rows).astype(jnp.bfloat16)
        mixed_rows = gather_cfg(mixed_rows, active)
        projected = jnp.dot(
            mixed_rows.reshape(-1, width), qkv_full, preferred_element_type=jnp.float32
        )
        projected = projected.reshape(seq_count, patches, patch_dev, 3, group_heads, HD)
        projected = projected.transpose(0, 4, 3, 1, 2, 5)
        queries = rotate(head_norm(projected[:, :, 0]), cos_table, sin_table)
        key_part = rotate(head_norm(projected[:, :, 1]), cos_table, sin_table)
        stacked = jnp.stack([queries, key_part, projected[:, :, 2]], axis=2).astype(jnp.bfloat16)
        outgoing = stacked.reshape(seq_count * group_heads, 3, patches, patch_dev * HD)
        incoming = lax.all_to_all(outgoing, "seq", split_axis=0, concat_axis=3, tiled=True)
        incoming = incoming.reshape(3, patches, patch_len, HD)
        fresh_rows = jnp.concatenate([incoming[1], incoming[2]], axis=-1).reshape(
            total_len, 2 * HD
        )
        attended = attend(incoming[0], fresh_rows, stale_rows, live_flags)
        attended = attended.reshape(patches, seq_devices, patch_dev * HD)[None]
        returned = lax.all_to_all(attended, "seq", split_axis=2, concat_axis=0, tiled=True)
        returned = returned.reshape(seq_count, group_heads, patches, patch_dev, HD)
        update = scatter_cfg(
            jnp.einsum("sgpqe,dge->spqd", returned, out_full, preferred_element_type=jnp.float32),
            active,
        )
        result = (hidden.astype(jnp.float32) + gate_rows * update).astype(jnp.bfloat16)
        return result, fresh_rows

    first_out, first_cache = run(hidden_states, 0)
    received = from_behind(first_out, "section", 1)
    second_out, second_cache = run(received, 1)
    key_cache = jnp.where(section_id == 0, first_cache, second_cache)

    normed = row_norm(second_out.astype(jnp.float32))
    normed_out = (normed * (1.0 + out_modulation[1]) + out_modulation[0]).astype(jnp.bfloat16)
    predicted = jnp.einsum(
        "spqd,do->spqo", normed_out, proj_weight, preferred_element_type=jnp.float32
    )
    count = cfg_devices
    here = lax.axis_index("cfg")
    slots = []
    for step in range(count):
        pairs = [(count, step), (count + 1, (step + 1) % count)]
        if step < count - 1:
            pairs += [(count + 2, count + (3 + step) % count), (count + 3, count + step)]
        slots.append(lax.ppermute(predicted, ("section", "cfg"), pairs))
    slots = jnp.concatenate(slots, axis=0)
    first_table = jnp.array([1, 2, 0, 0], jnp.int32)
    second_table = jnp.array([0, 1, 2, 0], jnp.int32)
    first_at = jnp.where(section_id == 0, here, first_table[here])
    second_at = jnp.where(section_id == 0, (here + count - 1) % count, second_table[here])
    first_rows = lax.dynamic_index_in_dim(slots, first_at, 0, keepdims=False)
    second_rows = lax.dynamic_index_in_dim(slots, second_at, 0, keepdims=False)
    first_rows = jnp.where((section_id == 1) & (here == 2), predicted[0], first_rows)
    second_rows = jnp.where((section_id == 1) & (here == 3), predicted[0], second_rows)
    pair_rows = jnp.stack([first_rows, second_rows], axis=0)
    solver_row = solver_coef[0]
    guided = pair_rows[0] + solver_row[2] * (pair_rows[1] - pair_rows[0])
    new_latent = solver_row[0] * latent[0] + solver_row[1] * guided
    return (new_latent[None], key_cache[None, None, None])


def solution(mesh):
    return jax.shard_map(
        per_device,
        mesh=mesh,
        in_specs=(
            P("cfg", None, "seq", None),
            P("section", None, "seq", None),
            P("section", "cfg", "seq", None, None),
            P("section", None, None, "cfg"),
            P("section", "seq", "cfg"),
            P("section", None, None),
            P(),
            P(),
            P("section", None),
            P(),
            P(),
            P(None, None, None, "seq"),
        ),
        out_specs=(P("section", None, "seq", None), P("section", "cfg", "seq", None, None)),
        check_vma=False,
    )
```

```python
import math

import jax
import jax.numpy as jnp
from jax import lax
from jax.experimental import pallas as pl
from jax.sharding import PartitionSpec as P

HD = 64
TEXT = 226


def from_behind(value, axis, steps):
    count = lax.axis_size(axis)
    pairs = [(source, (source + steps) % count) for source in range(count)]
    return lax.ppermute(value, axis, pairs)


def row_norm(values):
    centered = values - jnp.mean(values, axis=-1, keepdims=True)
    return centered * lax.rsqrt(jnp.mean(centered * centered, axis=-1, keepdims=True) + 1e-05)


def head_norm(values):
    centered = values - jnp.mean(values, axis=-1, keepdims=True)
    return centered * lax.rsqrt(jnp.mean(centered * centered, axis=-1, keepdims=True) + 1e-06)


def rope_angles(places, head_size):
    half_size = head_size // 2
    pairs_t = head_size // 8
    pairs_h = (half_size - pairs_t) // 2
    pair_index = jnp.arange(half_size)
    first_part = pair_index < pairs_t
    second_part = jnp.logical_and(pair_index >= pairs_t, pair_index < pairs_t + pairs_h)
    third_part = pair_index >= pairs_t + pairs_h
    local_index = jnp.where(
        first_part,
        pair_index,
        jnp.where(second_part, pair_index - pairs_t, pair_index - pairs_t - pairs_h),
    )
    axis_span = jnp.where(first_part, 2 * pairs_t, 2 * pairs_h)
    frequency = jnp.exp(
        -math.log(10000.0) * 2.0 * local_index.astype(jnp.float32) / axis_span.astype(jnp.float32)
    )
    angles = places[0][..., None] * first_part.astype(jnp.float32)
    angles = angles + places[1][..., None] * second_part.astype(jnp.float32)
    angles = angles + places[2][..., None] * third_part.astype(jnp.float32)
    return angles * frequency


def rotate(values, cos_table, sin_table):
    half_size = values.shape[-1] // 2
    first_half = values[..., :half_size]
    second_half = values[..., half_size:]
    return jnp.concatenate(
        [
            first_half * cos_table - second_half * sin_table,
            second_half * cos_table + first_half * sin_table,
        ],
        axis=-1,
    )


def shift_within(value, active, steps):
    count = lax.axis_size("cfg")
    pairs = [
        (active * count + source, active * count + (source + steps) % count)
        for source in range(count)
    ]
    return lax.ppermute(value, ("section", "cfg"), pairs)


def gather_cfg(values, active):
    count = lax.axis_size("cfg")
    here = lax.axis_index("cfg")
    slots = [values] + [shift_within(values, active, shift) for shift in range(1, count)]
    ordered = jnp.concatenate(slots[::-1], axis=0)
    return jnp.roll(ordered, here + 1, axis=0)


def scatter_cfg(partials, active):
    count = lax.axis_size("cfg")
    here = lax.axis_index("cfg")
    total = lax.dynamic_index_in_dim(partials, here, 0, keepdims=True)
    for shift in range(1, count):
        outgoing = lax.dynamic_index_in_dim(partials, (here + shift) % count, 0, keepdims=True)
        outgoing = outgoing.astype(jnp.bfloat16)
        total = total + shift_within(outgoing, active, shift).astype(jnp.float32)
    return total


def attend_kernel(query_ref, fresh_key_ref, fresh_value_ref, stale_key_ref, stale_value_ref, live_ref, out_ref):
    patch_id = pl.program_id(0) // 2
    patch_len = 2 * query_ref.shape[1]
    total_len = fresh_key_ref.shape[0]
    key_patch = lax.broadcasted_iota(jnp.int32, (total_len, 1), 0) // patch_len
    use_fresh = key_patch <= patch_id
    key_rows = jnp.where(use_fresh, fresh_key_ref[...], stale_key_ref[...])
    value_rows = jnp.where(use_fresh, fresh_value_ref[...], stale_value_ref[...])
    scores = lax.dot_general(
        query_ref[0] * jnp.asarray(HD ** (-0.5), query_ref.dtype),
        key_rows,
        (((1,), (1,)), ((), ())),
        preferred_element_type=jnp.float32,
    )
    scores = jnp.where(live_ref[...] > 0, scores, -jnp.inf)
    row_max = jnp.max(scores, axis=1, keepdims=True)
    weights = jnp.exp(scores - row_max)
    row_sum = jnp.sum(weights, axis=1, keepdims=True)
    combined = jnp.dot(
        weights.astype(jnp.bfloat16), value_rows, preferred_element_type=jnp.float32
    )
    out_ref[0] = (combined / row_sum).astype(out_ref.dtype)


def attend(queries, fresh_keys, fresh_values, stale_keys, stale_values, live_flags):
    patches, patch_len, head_size = queries.shape
    total_len = fresh_keys.shape[0]
    return pl.pallas_call(
        attend_kernel,
        grid=(2 * patches,),
        in_specs=[
            pl.BlockSpec((1, patch_len // 2, head_size), lambda p: (p // 2, p % 2, 0)),
            pl.BlockSpec((total_len, head_size), lambda p: (0, 0)),
            pl.BlockSpec((total_len, head_size), lambda p: (0, 0)),
            pl.BlockSpec((total_len, head_size), lambda p: (0, 0)),
            pl.BlockSpec((total_len, head_size), lambda p: (0, 0)),
            pl.BlockSpec((1, total_len), lambda p: (0, 0)),
        ],
        out_specs=pl.BlockSpec((1, patch_len // 2, head_size), lambda p: (p // 2, p % 2, 0)),
        out_shape=jax.ShapeDtypeStruct(queries.shape, jnp.bfloat16),
    )(queries, fresh_keys, fresh_values, stale_keys, stale_values, live_flags)


def per_device(
    hidden_states,
    latent,
    stale_cache,
    qkv_weight,
    out_weight,
    modulation,
    out_modulation,
    proj_weight,
    solver_coef,
    video_len,
    text_len,
    positions,
):
    section_id = lax.axis_index("section")
    shard_id = lax.axis_index("seq")
    seq_devices = lax.axis_size("seq")
    cfg_devices = lax.axis_size("cfg")
    patches = hidden_states.shape[1]
    patch_dev = hidden_states.shape[2]
    width = hidden_states.shape[3]
    patch_len = patch_dev * seq_devices
    total_len = patch_len * patches
    group_heads = qkv_weight.shape[3] // HD
    seq_count = cfg_devices
    qkv_full = qkv_weight[0].reshape(width, 3 * group_heads * HD)
    out_full = lax.all_gather(out_weight[0], "seq", axis=0, tiled=True).reshape(
        width, group_heads, HD
    )
    mod_rows = modulation[0]
    stale_rows = stale_cache[0, 0, 0]
    stale_keys = stale_rows[:, :HD]
    stale_values = stale_rows[:, HD:]
    my_sequence = shard_id // group_heads
    row_ids = jnp.arange(total_len)
    text_limit = lax.dynamic_index_in_dim(text_len, my_sequence, keepdims=False)
    video_limit = lax.dynamic_index_in_dim(video_len, my_sequence // 2, keepdims=False)
    live_keys = jnp.where(row_ids < TEXT, row_ids < text_limit, row_ids - TEXT < video_limit)
    live_flags = live_keys.astype(jnp.int32)[None, :]
    scale_factor = HD ** (-0.5)

    row_place = (
        jnp.arange(patches)[:, None] * patch_len
        + shard_id * patch_dev
        + jnp.arange(patch_dev)[None, :]
    )
    text_rows = (row_place < TEXT)[:, :, None]
    shift_rows = jnp.where(text_rows, mod_rows[3], mod_rows[0])
    scale_rows = jnp.where(text_rows, mod_rows[4], mod_rows[1])
    gate_rows = jnp.where(text_rows, mod_rows[5], mod_rows[2])
    angles = rope_angles(positions.astype(jnp.float32), HD)
    angles = jnp.where(text_rows[None], 0.0, angles)
    angles = jnp.repeat(angles, 2, axis=0)[:, None]
    cos_table = jnp.cos(angles)
    sin_table = jnp.sin(angles)

    def run(hidden, active):
        normed = row_norm(hidden.astype(jnp.float32))
        mixed_rows = (normed * (1.0 + scale_rows) + shift_rows).astype(jnp.bfloat16)
        mixed_rows = gather_cfg(mixed_rows, active)
        projected = jnp.dot(
            mixed_rows.reshape(-1, width), qkv_full, preferred_element_type=jnp.float32
        )
        projected = projected.reshape(seq_count, patches, patch_dev, 3, group_heads, HD)
        projected = projected.transpose(0, 4, 3, 1, 2, 5)
        queries = rotate(head_norm(projected[:, :, 0]), cos_table, sin_table)
        key_part = rotate(head_norm(projected[:, :, 1]), cos_table, sin_table)
        stacked = jnp.stack([queries, key_part, projected[:, :, 2]], axis=2).astype(jnp.bfloat16)
        outgoing = stacked.reshape(seq_count * group_heads, 3, patches, patch_dev * HD)
        incoming = lax.all_to_all(outgoing, "seq", split_axis=0, concat_axis=3, tiled=True)
        incoming = incoming.reshape(3, patches, patch_len, HD)
        fresh_rows = jnp.concatenate([incoming[1], incoming[2]], axis=-1).reshape(
            total_len, 2 * HD
        )
        attended = attend(
            incoming[0],
            incoming[1].reshape(total_len, HD),
            incoming[2].reshape(total_len, HD),
            stale_keys,
            stale_values,
            live_flags,
        )
        attended = attended.reshape(patches, seq_devices, patch_dev * HD)[None]
        returned = lax.all_to_all(attended, "seq", split_axis=2, concat_axis=0, tiled=True)
        returned = returned.reshape(seq_count, group_heads, patches, patch_dev, HD)
        update = scatter_cfg(
            jnp.einsum("sgpqe,dge->spqd", returned, out_full, preferred_element_type=jnp.float32),
            active,
        )
        result = (hidden.astype(jnp.float32) + gate_rows * update).astype(jnp.bfloat16)
        return result, fresh_rows

    first_out, first_cache = run(hidden_states, 0)
    received = from_behind(first_out, "section", 1)
    second_out, second_cache = run(received, 1)
    key_cache = jnp.where(section_id == 0, first_cache, second_cache)

    normed = row_norm(second_out.astype(jnp.float32))
    normed_out = (normed * (1.0 + out_modulation[1]) + out_modulation[0]).astype(jnp.bfloat16)
    predicted = jnp.einsum(
        "spqd,do->spqo", normed_out, proj_weight, preferred_element_type=jnp.float32
    )
    count = cfg_devices
    here = lax.axis_index("cfg")
    slots = []
    for step in range(count):
        pairs = [(count, step), (count + 1, (step + 1) % count)]
        if step < count - 1:
            pairs += [(count + 2, count + (3 + step) % count), (count + 3, count + step)]
        slots.append(lax.ppermute(predicted, ("section", "cfg"), pairs))
    slots = jnp.concatenate(slots, axis=0)
    first_table = jnp.array([1, 2, 0, 0], jnp.int32)
    second_table = jnp.array([0, 1, 2, 0], jnp.int32)
    first_at = jnp.where(section_id == 0, here, first_table[here])
    second_at = jnp.where(section_id == 0, (here + count - 1) % count, second_table[here])
    first_rows = lax.dynamic_index_in_dim(slots, first_at, 0, keepdims=False)
    second_rows = lax.dynamic_index_in_dim(slots, second_at, 0, keepdims=False)
    first_rows = jnp.where((section_id == 1) & (here == 2), predicted[0], first_rows)
    second_rows = jnp.where((section_id == 1) & (here == 3), predicted[0], second_rows)
    pair_rows = jnp.stack([first_rows, second_rows], axis=0)
    solver_row = solver_coef[0]
    guided = pair_rows[0] + solver_row[2] * (pair_rows[1] - pair_rows[0])
    new_latent = solver_row[0] * latent[0] + solver_row[1] * guided
    return (new_latent[None], key_cache[None, None, None])


def solution(mesh):
    return jax.shard_map(
        per_device,
        mesh=mesh,
        in_specs=(
            P("cfg", None, "seq", None),
            P("section", None, "seq", None),
            P("section", "cfg", "seq", None, None),
            P("section", None, None, "cfg"),
            P("section", "seq", "cfg"),
            P("section", None, None),
            P(),
            P(),
            P("section", None),
            P(),
            P(),
            P(None, None, None, "seq"),
        ),
        out_specs=(P("section", None, "seq", None), P("section", "cfg", "seq", None, None)),
        check_vma=False,
    )
```

```python
import math

import jax
import jax.numpy as jnp
from jax import lax
from jax.experimental import pallas as pl
from jax.sharding import PartitionSpec as P

HD = 64
TEXT = 226


def from_behind(value, axis, steps):
    count = lax.axis_size(axis)
    pairs = [(source, (source + steps) % count) for source in range(count)]
    return lax.ppermute(value, axis, pairs)


def row_norm(values):
    centered = values - jnp.mean(values, axis=-1, keepdims=True)
    return centered * lax.rsqrt(jnp.mean(centered * centered, axis=-1, keepdims=True) + 1e-05)


def head_norm(values):
    centered = values - jnp.mean(values, axis=-1, keepdims=True)
    return centered * lax.rsqrt(jnp.mean(centered * centered, axis=-1, keepdims=True) + 1e-06)


def rope_angles(places, head_size):
    half_size = head_size // 2
    pairs_t = head_size // 8
    pairs_h = (half_size - pairs_t) // 2
    pair_index = jnp.arange(half_size)
    first_part = pair_index < pairs_t
    second_part = jnp.logical_and(pair_index >= pairs_t, pair_index < pairs_t + pairs_h)
    third_part = pair_index >= pairs_t + pairs_h
    local_index = jnp.where(
        first_part,
        pair_index,
        jnp.where(second_part, pair_index - pairs_t, pair_index - pairs_t - pairs_h),
    )
    axis_span = jnp.where(first_part, 2 * pairs_t, 2 * pairs_h)
    frequency = jnp.exp(
        -math.log(10000.0) * 2.0 * local_index.astype(jnp.float32) / axis_span.astype(jnp.float32)
    )
    angles = places[0][..., None] * first_part.astype(jnp.float32)
    angles = angles + places[1][..., None] * second_part.astype(jnp.float32)
    angles = angles + places[2][..., None] * third_part.astype(jnp.float32)
    return angles * frequency


def rotate(values, cos_table, sin_table):
    half_size = values.shape[-1] // 2
    first_half = values[..., :half_size]
    second_half = values[..., half_size:]
    return jnp.concatenate(
        [
            first_half * cos_table - second_half * sin_table,
            second_half * cos_table + first_half * sin_table,
        ],
        axis=-1,
    )


def shift_within(value, active, steps):
    count = lax.axis_size("cfg")
    pairs = [
        (active * count + source, active * count + (source + steps) % count)
        for source in range(count)
    ]
    return lax.ppermute(value, ("section", "cfg"), pairs)


def gather_cfg(values, active):
    count = lax.axis_size("cfg")
    here = lax.axis_index("cfg")
    slots = [values] + [shift_within(values, active, shift) for shift in range(1, count)]
    ordered = jnp.concatenate(slots[::-1], axis=0)
    return jnp.roll(ordered, here + 1, axis=0)


def scatter_cfg(partials, active):
    count = lax.axis_size("cfg")
    here = lax.axis_index("cfg")
    total = lax.dynamic_index_in_dim(partials, here, 0, keepdims=True)
    for shift in range(1, count):
        outgoing = lax.dynamic_index_in_dim(partials, (here + shift) % count, 0, keepdims=True)
        outgoing = outgoing.astype(jnp.bfloat16)
        total = total + shift_within(outgoing, active, shift).astype(jnp.float32)
    return total


def attend_kernel(query_ref, fresh_key_ref, fresh_value_ref, stale_key_ref, stale_value_ref, live_ref, out_ref):
    patch_id = pl.program_id(0) // 2
    patch_len = 2 * query_ref.shape[1]
    total_len = fresh_key_ref.shape[0]
    key_patch = lax.broadcasted_iota(jnp.int32, (total_len, 1), 0) // patch_len
    use_fresh = key_patch <= patch_id
    key_rows = jnp.where(use_fresh, fresh_key_ref[...], stale_key_ref[...])
    value_rows = jnp.where(use_fresh, fresh_value_ref[...], stale_value_ref[...])
    scores = lax.dot_general(
        query_ref[0] * jnp.asarray(HD ** (-0.5), query_ref.dtype),
        key_rows,
        (((1,), (1,)), ((), ())),
        preferred_element_type=jnp.float32,
    )
    scores = scores + live_ref[...]
    row_max = jnp.max(scores, axis=1, keepdims=True)
    weights = jnp.exp(scores - row_max)
    row_sum = jnp.sum(weights, axis=1, keepdims=True)
    combined = jnp.dot(
        weights.astype(jnp.bfloat16), value_rows, preferred_element_type=jnp.float32
    )
    out_ref[0] = (combined / row_sum).astype(out_ref.dtype)


def attend(queries, fresh_keys, fresh_values, stale_keys, stale_values, live_flags):
    patches, patch_len, head_size = queries.shape
    total_len = fresh_keys.shape[0]
    return pl.pallas_call(
        attend_kernel,
        grid=(2 * patches,),
        in_specs=[
            pl.BlockSpec((1, patch_len // 2, head_size), lambda p: (p // 2, p % 2, 0)),
            pl.BlockSpec((total_len, head_size), lambda p: (0, 0)),
            pl.BlockSpec((total_len, head_size), lambda p: (0, 0)),
            pl.BlockSpec((total_len, head_size), lambda p: (0, 0)),
            pl.BlockSpec((total_len, head_size), lambda p: (0, 0)),
            pl.BlockSpec((1, total_len), lambda p: (0, 0)),
        ],
        out_specs=pl.BlockSpec((1, patch_len // 2, head_size), lambda p: (p // 2, p % 2, 0)),
        out_shape=jax.ShapeDtypeStruct(queries.shape, jnp.bfloat16),
    )(queries, fresh_keys, fresh_values, stale_keys, stale_values, live_flags)


def per_device(
    hidden_states,
    latent,
    stale_cache,
    qkv_weight,
    out_weight,
    modulation,
    out_modulation,
    proj_weight,
    solver_coef,
    video_len,
    text_len,
    positions,
):
    section_id = lax.axis_index("section")
    shard_id = lax.axis_index("seq")
    seq_devices = lax.axis_size("seq")
    cfg_devices = lax.axis_size("cfg")
    patches = hidden_states.shape[1]
    patch_dev = hidden_states.shape[2]
    width = hidden_states.shape[3]
    patch_len = patch_dev * seq_devices
    total_len = patch_len * patches
    group_heads = qkv_weight.shape[3] // HD
    seq_count = cfg_devices
    qkv_full = qkv_weight[0].reshape(width, 3 * group_heads * HD)
    out_full = lax.all_gather(out_weight[0], "seq", axis=0, tiled=True).reshape(
        width, group_heads, HD
    )
    mod_rows = modulation[0]
    stale_rows = stale_cache[0, 0, 0]
    stale_keys = stale_rows[:, :HD]
    stale_values = stale_rows[:, HD:]
    my_sequence = shard_id // group_heads
    row_ids = jnp.arange(total_len)
    text_limit = lax.dynamic_index_in_dim(text_len, my_sequence, keepdims=False)
    video_limit = lax.dynamic_index_in_dim(video_len, my_sequence // 2, keepdims=False)
    live_keys = jnp.where(row_ids < TEXT, row_ids < text_limit, row_ids - TEXT < video_limit)
    live_flags = jnp.where(live_keys, 0.0, -jnp.inf).astype(jnp.float32)[None, :]
    scale_factor = HD ** (-0.5)

    row_place = (
        jnp.arange(patches)[:, None] * patch_len
        + shard_id * patch_dev
        + jnp.arange(patch_dev)[None, :]
    )
    text_rows = (row_place < TEXT)[:, :, None]
    shift_rows = jnp.where(text_rows, mod_rows[3], mod_rows[0])
    scale_rows = jnp.where(text_rows, mod_rows[4], mod_rows[1])
    gate_rows = jnp.where(text_rows, mod_rows[5], mod_rows[2])
    angles = rope_angles(positions.astype(jnp.float32), HD)
    angles = jnp.where(text_rows[None], 0.0, angles)
    angles = jnp.repeat(angles, 2, axis=0)[:, None]
    cos_table = jnp.cos(angles)
    sin_table = jnp.sin(angles)

    def run(hidden, active):
        normed = row_norm(hidden.astype(jnp.float32))
        mixed_rows = (normed * (1.0 + scale_rows) + shift_rows).astype(jnp.bfloat16)
        mixed_rows = gather_cfg(mixed_rows, active)
        projected = jnp.dot(
            mixed_rows.reshape(-1, width), qkv_full, preferred_element_type=jnp.float32
        )
        projected = projected.reshape(seq_count, patches, patch_dev, 3, group_heads, HD)
        projected = projected.transpose(0, 4, 3, 1, 2, 5)
        queries = rotate(head_norm(projected[:, :, 0]), cos_table, sin_table)
        key_part = rotate(head_norm(projected[:, :, 1]), cos_table, sin_table)
        stacked = jnp.stack([queries, key_part, projected[:, :, 2]], axis=2).astype(jnp.bfloat16)
        outgoing = stacked.reshape(seq_count * group_heads, 3, patches, patch_dev * HD)
        incoming = lax.all_to_all(outgoing, "seq", split_axis=0, concat_axis=3, tiled=True)
        incoming = incoming.reshape(3, patches, patch_len, HD)
        fresh_rows = jnp.concatenate([incoming[1], incoming[2]], axis=-1).reshape(
            total_len, 2 * HD
        )
        attended = attend(
            incoming[0],
            incoming[1].reshape(total_len, HD),
            incoming[2].reshape(total_len, HD),
            stale_keys,
            stale_values,
            live_flags,
        )
        attended = attended.reshape(patches, seq_devices, patch_dev * HD)[None]
        returned = lax.all_to_all(attended, "seq", split_axis=2, concat_axis=0, tiled=True)
        returned = returned.reshape(seq_count, group_heads, patches, patch_dev, HD)
        update = scatter_cfg(
            jnp.einsum("sgpqe,dge->spqd", returned, out_full, preferred_element_type=jnp.float32),
            active,
        )
        result = (hidden.astype(jnp.float32) + gate_rows * update).astype(jnp.bfloat16)
        return result, fresh_rows

    first_out, first_cache = run(hidden_states, 0)
    received = from_behind(first_out, "section", 1)
    second_out, second_cache = run(received, 1)
    key_cache = jnp.where(section_id == 0, first_cache, second_cache)

    normed = row_norm(second_out.astype(jnp.float32))
    normed_out = (normed * (1.0 + out_modulation[1]) + out_modulation[0]).astype(jnp.bfloat16)
    predicted = jnp.einsum(
        "spqd,do->spqo", normed_out, proj_weight, preferred_element_type=jnp.float32
    )
    count = cfg_devices
    here = lax.axis_index("cfg")
    slots = []
    for step in range(count):
        pairs = [(count, step), (count + 1, (step + 1) % count)]
        if step < count - 1:
            pairs += [(count + 2, count + (3 + step) % count), (count + 3, count + step)]
        slots.append(lax.ppermute(predicted, ("section", "cfg"), pairs))
    slots = jnp.concatenate(slots, axis=0)
    first_table = jnp.array([1, 2, 0, 0], jnp.int32)
    second_table = jnp.array([0, 1, 2, 0], jnp.int32)
    first_at = jnp.where(section_id == 0, here, first_table[here])
    second_at = jnp.where(section_id == 0, (here + count - 1) % count, second_table[here])
    first_rows = lax.dynamic_index_in_dim(slots, first_at, 0, keepdims=False)
    second_rows = lax.dynamic_index_in_dim(slots, second_at, 0, keepdims=False)
    first_rows = jnp.where((section_id == 1) & (here == 2), predicted[0], first_rows)
    second_rows = jnp.where((section_id == 1) & (here == 3), predicted[0], second_rows)
    pair_rows = jnp.stack([first_rows, second_rows], axis=0)
    solver_row = solver_coef[0]
    guided = pair_rows[0] + solver_row[2] * (pair_rows[1] - pair_rows[0])
    new_latent = solver_row[0] * latent[0] + solver_row[1] * guided
    return (new_latent[None], key_cache[None, None, None])


def solution(mesh):
    return jax.shard_map(
        per_device,
        mesh=mesh,
        in_specs=(
            P("cfg", None, "seq", None),
            P("section", None, "seq", None),
            P("section", "cfg", "seq", None, None),
            P("section", None, None, "cfg"),
            P("section", "seq", "cfg"),
            P("section", None, None),
            P(),
            P(),
            P("section", None),
            P(),
            P(),
            P(None, None, None, "seq"),
        ),
        out_specs=(P("section", None, "seq", None), P("section", "cfg", "seq", None, None)),
        check_vma=False,
    )
```
